256 devices in a mesh: lat: 8 (over y_hi, x), lon: 32 (over y_lo, z, core).
Axes of the slice: x: 4, y: 4 (y_hi: 2, y_lo: 2; y = y_hi * 2 + y_lo), z: 8, core: 2. Of those that a mesh axis runs over, the one named last changes fastest.
Arguments:
- feat_one: bfloat16 [128, 2048, 256], P('lat', 'lon'), may hold values from -6 to 6
- feat_two: bfloat16 [128, 2048, 256], P('lat', 'lon'), may hold values from -6 to 6
- context_in: bfloat16 [128, 2048, 128], P('lat', 'lon'), may hold values from 0 to 2
- hidden_init: bfloat16 [128, 2048, 128], P('lat', 'lon'), may hold values from -1 to 1
- corr_proj: bfloat16 [8, 128, 128], replicated, may hold values from -0.5 to 0.5
- input_conv: bfloat16 [2, 5, 256, 384], replicated, may hold values from -0.125 to 0.125
- state_zr: bfloat16 [2, 5, 128, 256], replicated, may hold values from -0.75 to 0.75
- state_q: bfloat16 [2, 5, 128, 128], replicated, may hold values from -0.75 to 0.75
- update_bias: float32 [2, 128], replicated, may hold values from -2 to 0
- gate_bias: float32 [2, 256], replicated, may hold values from -3 to 3
- blk_offset: int32 [8, 32, 12], P('lat', 'lon'), may hold values from -4 to 4, as said below
- blk_class: int32 [8, 32, 12], P('lat', 'lon'), may hold values from 0 to 7
- blk_count: int32 [8, 32], P('lat', 'lon'), may hold values from 1 to 12, as said below
Outputs:
- hidden: bfloat16 [128, 2048, 128], P('lat', 'lon')
The draws below stay inside these ranges and needn't reach their ends.
Inputs may be any that keep to these rules, and one draw needn't show every extreme that they name: `blk_offset`: offsets of panels along the closed longitude loop; bands nearer a pole reach farther, the bands at the poles up to 4 either way, and both ends are reached in every draw. Slots at or beyond blk_count are unused. `blk_count`: bands nearer a pole hold more live slots; some panel of the first band holds 12.
All inputs are finite; a program needn't handle non-finite values.
Results may differ from the reference program's by a relative error of at most 0.019.
Values may be sent and summed in bfloat16 or wider, within the bound.
No kernel may reach another device: no remote copies, remote signals or barrier semaphores. Data moves between devices by JAX's collectives and lax.ppermute only.
A program may use at most 64 MiB of HBM per device.

```python
import jax
import jax.numpy as jnp
from jax import lax

C = 256
H = 128
ROWS = 16
COLS = 64
POOLR = 8
POOLC = 16
MAXB = 12
RMAX = 4
NCLASS = 8
ITERS = 4
NLAT = 128
NLON = 2048
N_LAT = 8
N_LON = 32


def forced_column(key):
    return jax.random.randint(jax.random.fold_in(key, 7), (), 0, N_LON)


def band_distance():
    latitude = jnp.arange(N_LAT, dtype=jnp.int32)
    return jnp.abs(2 * latitude + 1 - N_LAT)


def draw_blk_count(key, part):
    distance = band_distance()
    denom = max((N_LAT - 1) ** 2, 1)
    top = 2 + (MAXB - 2) * distance * distance // denom
    lowest = jnp.maximum(top - 2, 1)
    extra = jax.random.randint(jax.random.fold_in(key, 1), (N_LAT, N_LON), 0, 3)
    counts = jnp.minimum(lowest[:, None] + extra, MAXB)
    counts = counts.at[0, forced_column(key)].set(MAXB)
    return counts.astype(jnp.int32)


def draw_blk_offset(key, part):
    distance = band_distance()
    denom = max((N_LAT - 1) ** 2, 1)
    reach = 1 + (RMAX - 1) * distance * distance // denom
    raw = jax.random.randint(jax.random.fold_in(key, 2), (N_LAT, N_LON, MAXB), 0, 2 * RMAX + 1)
    offsets = raw % (2 * reach[:, None, None] + 1) - reach[:, None, None]
    column = forced_column(key)
    offsets = offsets.at[0, column, 0].set(RMAX)
    offsets = offsets.at[0, column, 1].set(-RMAX)
    return offsets.astype(jnp.int32)


def draw_hidden_init(key, part):
    shape = (NLAT, NLON, H)
    values = jax.random.uniform(jax.random.fold_in(key, 11), shape, jnp.float32, -1.0, 1.0)
    return values.astype(jnp.bfloat16)


def place_ends(drawn, own_key, smallest, top_value):
    shape = drawn.shape
    spot = [jax.random.randint(jax.random.fold_in(own_key, axis), (), 0, shape[axis]) for axis in range(len(shape))]
    drawn = drawn.at[tuple(spot)].set(smallest)
    longest = shape.index(max(shape))
    spot[longest] = (spot[longest] + 1) % shape[longest]
    return drawn.at[tuple(spot)].set(top_value)


def levels(rng, extent, split, low, high):
    level = 1.0
    for position, parts in split:
        heights = jax.random.uniform(jax.random.fold_in(jax.random.fold_in(rng, 6), position), (parts,), jnp.float32, low / len(split), high / len(split))
        level = level * jnp.repeat(jnp.exp(heights), extent[position] // parts).reshape((-1,) + (1,) * (len(extent) - 1 - position))
    return level


def bell_draw(key, extent, scale, most, split=(), kind=jnp.bfloat16):
    loudness = levels(key, extent, split, -0.22, 0.18) if split else 1.0
    result = jax.random.normal(key, extent, jnp.float32) * scale * loudness
    return jnp.minimum(jnp.maximum(result, -most), most).astype(kind)


def setup_inputs(seed: int = 0) -> dict:
    seeds = jax.random.split(jax.random.key(seed), 14)
    return {
        "feat_one": bell_draw(seeds[0], (NLAT, NLON, C), 1.0, 6.0, ((0, 8), (1, 32))),
        "feat_two": bell_draw(seeds[1], (NLAT, NLON, C), 1.0, 6.0, ((0, 8), (1, 32))),
        "context_in": jnp.clip(2.0 * jax.random.uniform(seeds[2], (NLAT, NLON, H), jnp.float32) ** levels(seeds[2], (NLAT, NLON, H), ((0, 8), (1, 32)), -0.2, 0.2), 0.0, 2.0).astype(jnp.bfloat16),
        "hidden_init": draw_hidden_init(jax.random.fold_in(seeds[13], 71), 0),
        "corr_proj": bell_draw(seeds[4], (NCLASS, POOLR * POOLC, H), (POOLR * POOLC) ** -0.5, 0.5),
        "input_conv": bell_draw(seeds[5], (2, 5, 2 * H, 3 * H), (15 * H) ** -0.5, 0.125),
        "state_zr": bell_draw(seeds[6], (2, 5, H, 2 * H), (H // 2) ** -0.5, 0.75),
        "state_q": bell_draw(seeds[7], (2, 5, H, H), (H // 2) ** -0.5, 0.75),
        "update_bias": jnp.clip(jax.random.uniform(seeds[8], (2, H), jnp.float32, -2.0, 0.0), -2.0, 0.0),
        "gate_bias": bell_draw(seeds[9], (2, 2 * H), 0.5, 3.0, (), jnp.float32),
        "blk_offset": draw_blk_offset(jax.random.fold_in(seeds[13], 71), 0),
        "blk_class": place_ends(jax.random.randint(seeds[11], (N_LAT, N_LON, MAXB), 0, NCLASS), jax.random.fold_in(seeds[11], 1), 0, NCLASS - 1).astype(jnp.int32),
        "blk_count": draw_blk_count(jax.random.fold_in(seeds[13], 71), 0),
    }


def conv_lon(values, weight):
    width = values.shape[1]
    padded = jnp.concatenate([values[:, width - 2:], values, values[:, :2]], axis=1)
    total = jnp.zeros((values.shape[0] * width, weight.shape[2]), jnp.float32)
    for tap in range(5):
        piece = padded[:, tap:tap + width].reshape(-1, values.shape[2])
        total = total + jnp.dot(piece, weight[tap], preferred_element_type=jnp.float32)
    return total


def conv_lat(values, weight):
    height = values.shape[0]
    padded = jnp.pad(values, ((2, 2), (0, 0), (0, 0)))
    total = jnp.zeros((height * values.shape[1], weight.shape[2]), jnp.float32)
    for tap in range(5):
        piece = padded[tap:tap + height].reshape(-1, values.shape[2])
        total = total + jnp.dot(piece, weight[tap], preferred_element_type=jnp.float32)
    return total


def gru_pass(state, inputs, conv, zr_weight, q_weight, z_bias, gate_row, shape):
    hid = state.shape[1]
    state_bf = state.astype(jnp.bfloat16).reshape(shape)
    mixed = conv(state_bf, zr_weight)
    update = jax.nn.sigmoid(inputs[:, :hid] + mixed[:, :hid] + z_bias)
    reset = jax.nn.sigmoid(inputs[:, hid:2 * hid] + mixed[:, hid:] + gate_row[:hid])
    reset_state = (reset * state).astype(jnp.bfloat16).reshape(shape)
    candidate = jnp.tanh(inputs[:, 2 * hid:] + conv(reset_state, q_weight) + gate_row[hid:])
    return (1.0 - update) * state + update * candidate


def reference(feat_one, feat_two, context_in, hidden_init, corr_proj, input_conv, state_zr, state_q, update_bias, gate_bias, blk_offset, blk_class, blk_count):
    pool_rows = ROWS // POOLR
    pool_cols = COLS // POOLC
    points = POOLR * POOLC

    def band_motion(inputs):
        first, second, offsets, classes, counts = inputs
        queries = first.reshape(ROWS, N_LON, COLS, C).transpose(1, 0, 2, 3).reshape(N_LON, ROWS * COLS, C).astype(jnp.float32)
        grid = second.reshape(POOLR, pool_rows, N_LON, POOLC, pool_cols, C)
        pooled = (jnp.sum(grid, axis=(1, 4), dtype=jnp.float32) / (pool_rows * pool_cols)).astype(jnp.bfloat16)
        pooled = pooled.transpose(1, 0, 2, 3).reshape(N_LON, points, C)
        panels = jnp.arange(N_LON, dtype=jnp.int32)
        total = jnp.zeros((N_LON, ROWS * COLS, H), jnp.float32)
        for slot in range(MAXB):
            target = ((panels + offsets[:, slot]) % N_LON).astype(jnp.int32)
            keys = jnp.take(pooled, target, axis=0).astype(jnp.float32)
            corr = (jnp.einsum("nqc,npc->nqp", queries, keys) * (C ** -0.5)).astype(jnp.bfloat16)
            proj = jnp.take(corr_proj, classes[:, slot], axis=0).astype(jnp.float32)
            term = jnp.einsum("nqp,nph->nqh", corr.astype(jnp.float32), proj)
            total = total + jnp.where((slot < counts)[:, None, None], term, jnp.float32(0.0))
        motion = jnp.maximum(total, 0.0).astype(jnp.bfloat16)
        return motion.reshape(N_LON, ROWS, COLS, H).transpose(1, 0, 2, 3).reshape(ROWS, N_LON * COLS, H)

    motion = lax.map(band_motion, (feat_one.reshape(N_LAT, ROWS, NLON, C), feat_two.reshape(N_LAT, ROWS, NLON, C), blk_offset, blk_class, blk_count))
    motion = motion.reshape(NLAT, NLON, H)
    joined = jnp.concatenate([context_in, motion], axis=2)
    x_lon = conv_lon(joined, input_conv[0])
    x_lat = conv_lat(joined, input_conv[1])
    shape = (NLAT, NLON, H)
    state = hidden_init.astype(jnp.float32).reshape(-1, H)
    for step in range(ITERS):
        state = gru_pass(state, x_lon, conv_lon, state_zr[0], state_q[0], update_bias[0], gate_bias[0], shape)
        state = gru_pass(state, x_lat, conv_lat, state_zr[1], state_q[1], update_bias[1], gate_bias[1], shape)
    return state.astype(jnp.bfloat16).reshape(shape)
```

```python
import jax
import jax.numpy as jnp
from jax import lax
from jax.sharding import PartitionSpec as P

POOLR = 8
POOLC = 16
RMAX = 4
ITERS = 4
NCLASS = 8
HALO = 4


def passed_along(value, axis, steps):
    count = lax.axis_size(axis)
    pairs = [(source, (source + steps) % count) for source in range(count)]
    return lax.ppermute(value, axis, pairs)


def extended(block, axis, dim, width, periodic):
    count = lax.axis_size(axis)
    forward = [(i, i + 1) for i in range(count - 1)]
    if periodic:
        forward.append((count - 1, 0))
    backward = [(target, source) for source, target in forward]
    low = lax.ppermute(
        lax.slice_in_dim(block, block.shape[dim] - width, None, axis=dim), axis, forward
    )
    high = lax.ppermute(lax.slice_in_dim(block, 0, width, axis=dim), axis, backward)
    return jnp.concatenate([low, block, high], axis=dim)


def rim_lon(values, width):
    return extended(values, "lon", 1, width, True)


def rim_lat(values, width):
    return extended(values, "lat", 0, width, False)


def valid_conv(padded, weight, dim, out_len):
    other = padded.shape[1 - dim]
    total = None
    for tap in range(5):
        piece = lax.slice_in_dim(padded, tap, tap + out_len, axis=dim).reshape(-1, padded.shape[2])
        term = jnp.dot(piece, weight[tap], preferred_element_type=jnp.float32)
        total = term if total is None else total + term
    if dim == 0:
        return total.reshape(out_len, other, -1)
    return total.reshape(other, out_len, -1)


def gru_pass(state, inputs, dim, rim, zr_weight, q_weight, z_bias, gate_row):
    hid = state.shape[2]
    size = state.shape[dim]
    inner = size + 2 * (HALO - 2)
    wide = rim(state, HALO)
    mixed = valid_conv(wide.astype(jnp.bfloat16), zr_weight, dim, inner)
    reset = jax.nn.sigmoid(inputs[..., hid : 2 * hid] + mixed[..., hid:] + gate_row[:hid])
    mid = lax.slice_in_dim(wide, 2, 2 + inner, axis=dim)
    reset_state = (reset * mid).astype(jnp.bfloat16)
    core_x = lax.slice_in_dim(inputs, HALO - 2, HALO - 2 + size, axis=dim)
    core_mixed = lax.slice_in_dim(mixed, HALO - 2, HALO - 2 + size, axis=dim)
    update = jax.nn.sigmoid(core_x[..., :hid] + core_mixed[..., :hid] + z_bias)
    candidate = jnp.tanh(
        core_x[..., 2 * hid :] + valid_conv(reset_state, q_weight, dim, size) + gate_row[hid:]
    )
    return (1.0 - update) * state + update * candidate


def local(
    feat_one,
    feat_two,
    context_in,
    hidden_init,
    corr_proj,
    input_conv,
    state_zr,
    state_q,
    update_bias,
    gate_bias,
    blk_offset,
    blk_class,
    blk_count,
):
    rows, cols, chans = feat_one.shape
    hid = hidden_init.shape[2]
    pool_rows = rows // POOLR
    pool_cols = cols // POOLC
    points = POOLR * POOLC
    grid = feat_two.reshape(POOLR, pool_rows, POOLC, pool_cols, chans)
    pooled = (jnp.sum(grid, axis=(1, 3), dtype=jnp.float32) / (pool_rows * pool_cols)).astype(
        jnp.bfloat16
    )
    pooled = pooled.reshape(points, chans)
    neighbours = []
    for step in range(-RMAX, RMAX + 1):
        if step == 0:
            neighbours.append(pooled)
        else:
            neighbours.append(passed_along(pooled, "lon", -step))
    keys = jnp.concatenate(neighbours, axis=0)

    queries = feat_one.reshape(rows * cols, chans)
    scale = chans ** (-0.5)
    corr = (
        lax.dot_general(queries, keys, (((1,), (1,)), ((), ())), preferred_element_type=jnp.float32)
        * scale
    ).astype(jnp.bfloat16)

    offsets = blk_offset[0, 0]
    classes = blk_class[0, 0]
    live = blk_count[0, 0]
    slots = offsets.shape[0]
    used = (jnp.arange(slots, dtype=jnp.int32) < live).astype(jnp.float32)
    by_offset = (offsets[None, :] + RMAX == jnp.arange(2 * RMAX + 1, dtype=jnp.int32)[:, None])
    by_class = classes[:, None] == jnp.arange(NCLASS, dtype=jnp.int32)[None, :]
    counts = jnp.dot(
        by_offset.astype(jnp.float32) * used[None, :],
        by_class.astype(jnp.float32),
        precision=lax.Precision.HIGHEST,
    )
    weight = jnp.einsum(
        "oc,cph->oph",
        counts.astype(jnp.bfloat16),
        corr_proj,
        preferred_element_type=jnp.float32,
    ).reshape((2 * RMAX + 1) * points, hid)
    weight_hi = weight.astype(jnp.bfloat16)
    weight_lo = (weight - weight_hi.astype(jnp.float32)).astype(jnp.bfloat16)
    both = jnp.dot(
        corr, jnp.concatenate([weight_hi, weight_lo], axis=1), preferred_element_type=jnp.float32
    )
    motion_sum = both[:, :hid] + both[:, hid:]
    motion = jnp.maximum(motion_sum, 0.0).astype(jnp.bfloat16).reshape(rows, cols, hid)
    joined = jnp.concatenate([context_in, motion], axis=2)
    x_lon = valid_conv(rim_lon(joined, HALO), input_conv[0], 1, cols + 2 * (HALO - 2))
    x_lat = valid_conv(rim_lat(joined, HALO), input_conv[1], 0, rows + 2 * (HALO - 2))
    state = hidden_init.astype(jnp.float32)
    for step in range(ITERS):
        state = gru_pass(
            state, x_lon, 1, rim_lon, state_zr[0], state_q[0], update_bias[0], gate_bias[0]
        )
        state = gru_pass(
            state, x_lat, 0, rim_lat, state_zr[1], state_q[1], update_bias[1], gate_bias[1]
        )
    return state.astype(jnp.bfloat16)


def solution(mesh):
    placed = (
        P("lat", "lon", None),
        P("lat", "lon", None),
        P("lat", "lon", None),
        P("lat", "lon", None),
        P(),
        P(),
        P(),
        P(),
        P(),
        P(),
        P("lat", "lon", None),
        P("lat", "lon", None),
        P("lat", "lon"),
    )
    return jax.shard_map(
        local, mesh=mesh, in_specs=placed, out_specs=P("lat", "lon", None), check_vma=False
    )
```

```python
import jax
import jax.numpy as jnp
from jax import lax
from jax.sharding import PartitionSpec as P

POOLR = 8
POOLC = 16
RMAX = 4
ITERS = 4
NCLASS = 8
HALO = 4


def passed_along(value, axis, steps):
    count = lax.axis_size(axis)
    pairs = [(source, (source + steps) % count) for source in range(count)]
    return lax.ppermute(value, axis, pairs)


def extended(block, axis, dim, width, periodic):
    count = lax.axis_size(axis)
    forward = [(i, i + 1) for i in range(count - 1)]
    if periodic:
        forward.append((count - 1, 0))
    backward = [(target, source) for source, target in forward]
    low = lax.ppermute(
        lax.slice_in_dim(block, block.shape[dim] - width, None, axis=dim), axis, forward
    )
    high = lax.ppermute(lax.slice_in_dim(block, 0, width, axis=dim), axis, backward)
    return jnp.concatenate([low, block, high], axis=dim)


def rim_lon(values, width):
    return extended(values, "lon", 0, width, True)


def rim_lat(values, width):
    return extended(values, "lat", 0, width, False)


def valid_conv(padded, weight, out_len):
    other = padded.shape[1]
    total = None
    for tap in range(5):
        piece = padded[tap : tap + out_len].reshape(-1, padded.shape[2])
        term = jnp.dot(piece, weight[tap], preferred_element_type=jnp.float32)
        total = term if total is None else total + term
    return total.reshape(out_len, other, -1)


def gru_pass(state, inputs, rim, zr_weight, q_weight, z_bias, gate_row):
    hid = state.shape[2]
    size = state.shape[0]
    inner = size + 2 * (HALO - 2)
    wide = rim(state, HALO)
    mixed = valid_conv(wide.astype(jnp.bfloat16), zr_weight, inner)
    reset = jax.nn.sigmoid(inputs[..., hid : 2 * hid] + mixed[..., hid:] + gate_row[:hid])
    reset_state = (reset * wide[2 : 2 + inner]).astype(jnp.bfloat16)
    core_x = inputs[HALO - 2 : HALO - 2 + size]
    core_mixed = mixed[HALO - 2 : HALO - 2 + size]
    update = jax.nn.sigmoid(core_x[..., :hid] + core_mixed[..., :hid] + z_bias)
    candidate = jnp.tanh(
        core_x[..., 2 * hid :] + valid_conv(reset_state, q_weight, size) + gate_row[hid:]
    )
    return (1.0 - update) * state + update * candidate


def local(
    feat_one,
    feat_two,
    context_in,
    hidden_init,
    corr_proj,
    input_conv,
    state_zr,
    state_q,
    update_bias,
    gate_bias,
    blk_offset,
    blk_class,
    blk_count,
):
    rows, cols, chans = feat_one.shape
    hid = hidden_init.shape[2]
    pool_rows = rows // POOLR
    pool_cols = cols // POOLC
    points = POOLR * POOLC
    cell = jnp.arange(rows * cols, dtype=jnp.int32)
    window = (cell // (cols * pool_rows)) * POOLC + (cell % cols) // pool_cols
    pool_mat = jnp.where(
        window[None, :] == jnp.arange(points, dtype=jnp.int32)[:, None],
        jnp.bfloat16(1.0 / (pool_rows * pool_cols)),
        jnp.bfloat16(0.0),
    )
    pooled = jnp.dot(
        pool_mat, feat_two.reshape(rows * cols, chans), preferred_element_type=jnp.float32
    ).astype(jnp.bfloat16)
    neighbours = []
    for step in range(-RMAX, RMAX + 1):
        if step == 0:
            neighbours.append(pooled)
        else:
            neighbours.append(passed_along(pooled, "lon", -step))
    keys = jnp.concatenate(neighbours, axis=0)

    queries = feat_one.reshape(rows * cols, chans)
    scale = chans ** (-0.5)
    corr = (
        lax.dot_general(queries, keys, (((1,), (1,)), ((), ())), preferred_element_type=jnp.float32)
        * scale
    ).astype(jnp.bfloat16)

    offsets = blk_offset[0, 0]
    classes = blk_class[0, 0]
    live = blk_count[0, 0]
    slots = offsets.shape[0]
    used = (jnp.arange(slots, dtype=jnp.int32) < live).astype(jnp.float32)
    by_offset = (offsets[None, :] + RMAX == jnp.arange(2 * RMAX + 1, dtype=jnp.int32)[:, None])
    by_class = classes[:, None] == jnp.arange(NCLASS, dtype=jnp.int32)[None, :]
    counts = jnp.dot(
        by_offset.astype(jnp.float32) * used[None, :],
        by_class.astype(jnp.float32),
        precision=lax.Precision.HIGHEST,
    )
    weight = jnp.einsum(
        "oc,cph->oph",
        counts.astype(jnp.bfloat16),
        corr_proj,
        preferred_element_type=jnp.float32,
    ).reshape((2 * RMAX + 1) * points, hid)
    weight_hi = weight.astype(jnp.bfloat16)
    weight_lo = (weight - weight_hi.astype(jnp.float32)).astype(jnp.bfloat16)
    both = jnp.dot(
        corr, jnp.concatenate([weight_hi, weight_lo], axis=1), preferred_element_type=jnp.float32
    )
    motion_sum = both[:, :hid] + both[:, hid:]
    motion = jnp.maximum(motion_sum, 0.0).astype(jnp.bfloat16).reshape(rows, cols, hid)
    joined = jnp.concatenate([context_in, motion], axis=2)
    x_lon = valid_conv(
        rim_lon(joined.transpose(1, 0, 2), HALO), input_conv[0], cols + 2 * (HALO - 2)
    )
    x_lat = valid_conv(rim_lat(joined, HALO), input_conv[1], rows + 2 * (HALO - 2))
    state = hidden_init.astype(jnp.float32)
    for step in range(ITERS):
        state = gru_pass(
            state.transpose(1, 0, 2),
            x_lon,
            rim_lon,
            state_zr[0],
            state_q[0],
            update_bias[0],
            gate_bias[0],
        ).transpose(1, 0, 2)
        state = gru_pass(
            state, x_lat, rim_lat, state_zr[1], state_q[1], update_bias[1], gate_bias[1]
        )
    return state.astype(jnp.bfloat16)


def solution(mesh):
    placed = (
        P("lat", "lon", None),
        P("lat", "lon", None),
        P("lat", "lon", None),
        P("lat", "lon", None),
        P(),
        P(),
        P(),
        P(),
        P(),
        P(),
        P("lat", "lon", None),
        P("lat", "lon", None),
        P("lat", "lon"),
    )
    return jax.shard_map(
        local, mesh=mesh, in_specs=placed, out_specs=P("lat", "lon", None), check_vma=False
    )
```

```python
import jax
import jax.numpy as jnp
from jax import lax
from jax.sharding import PartitionSpec as P

POOLR = 8
POOLC = 16
RMAX = 4
ITERS = 4
NCLASS = 8
HALO = 4


def passed_along(value, axis, steps):
    count = lax.axis_size(axis)
    pairs = [(source, (source + steps) % count) for source in range(count)]
    return lax.ppermute(value, axis, pairs)


def extended(block, axis, dim, width, periodic):
    count = lax.axis_size(axis)
    forward = [(i, i + 1) for i in range(count - 1)]
    if periodic:
        forward.append((count - 1, 0))
    backward = [(target, source) for source, target in forward]
    low = lax.ppermute(
        lax.slice_in_dim(block, block.shape[dim] - width, None, axis=dim), axis, forward
    )
    high = lax.ppermute(lax.slice_in_dim(block, 0, width, axis=dim), axis, backward)
    return jnp.concatenate([low, block, high], axis=dim)


def rim_lon(values, width):
    return extended(values, "lon", 0, width, True)


def rim_lat(values, width):
    count = lax.axis_size("lat")
    here = lax.axis_index("lat")
    forward = [(i, (i + 1) % count) for i in range(count)]
    backward = [(target, source) for source, target in forward]
    low = lax.ppermute(values[values.shape[0] - width :], "lat", forward)
    high = lax.ppermute(values[:width], "lat", backward)
    low = jnp.where(here > 0, low, jnp.zeros_like(low))
    high = jnp.where(here < count - 1, high, jnp.zeros_like(high))
    return jnp.concatenate([low, values, high], axis=0)


def valid_conv(padded, weight, out_len):
    other = padded.shape[1]
    total = None
    for tap in range(5):
        piece = padded[tap : tap + out_len].reshape(-1, padded.shape[2])
        term = jnp.dot(piece, weight[tap], preferred_element_type=jnp.float32)
        total = term if total is None else total + term
    return total.reshape(out_len, other, -1)


def gru_pass(state, inputs, rim, zr_weight, q_weight, z_bias, gate_row):
    hid = state.shape[2]
    size = state.shape[0]
    inner = size + 2 * (HALO - 2)
    wide = rim(state, HALO)
    mixed = valid_conv(wide.astype(jnp.bfloat16), zr_weight, inner)
    reset = jax.nn.sigmoid(inputs[..., hid : 2 * hid] + mixed[..., hid:] + gate_row[:hid])
    reset_state = (reset * wide[2 : 2 + inner]).astype(jnp.bfloat16)
    core_x = inputs[HALO - 2 : HALO - 2 + size]
    core_mixed = mixed[HALO - 2 : HALO - 2 + size]
    update = jax.nn.sigmoid(core_x[..., :hid] + core_mixed[..., :hid] + z_bias)
    candidate = jnp.tanh(
        core_x[..., 2 * hid :] + valid_conv(reset_state, q_weight, size) + gate_row[hid:]
    )
    return (1.0 - update) * state + update * candidate


def local(
    feat_one,
    feat_two,
    context_in,
    hidden_init,
    corr_proj,
    input_conv,
    state_zr,
    state_q,
    update_bias,
    gate_bias,
    blk_offset,
    blk_class,
    blk_count,
):
    rows, cols, chans = feat_one.shape
    hid = hidden_init.shape[2]
    pool_rows = rows // POOLR
    pool_cols = cols // POOLC
    points = POOLR * POOLC
    cell = jnp.arange(rows * cols, dtype=jnp.int32)
    window = (cell // (cols * pool_rows)) * POOLC + (cell % cols) // pool_cols
    pool_mat = jnp.where(
        window[None, :] == jnp.arange(points, dtype=jnp.int32)[:, None],
        jnp.bfloat16(1.0 / (pool_rows * pool_cols)),
        jnp.bfloat16(0.0),
    )
    pooled = jnp.dot(
        pool_mat, feat_two.reshape(rows * cols, chans), preferred_element_type=jnp.float32
    ).astype(jnp.bfloat16)
    near = jnp.concatenate(
        [passed_along(pooled, "lon", 1), pooled, passed_along(pooled, "lon", -1)], axis=0
    )
    reach = 3
    keys = jnp.concatenate(
        [passed_along(near, "lon", reach), near, passed_along(near, "lon", -reach)], axis=0
    )

    queries = feat_one.reshape(rows * cols, chans)
    scale = chans ** (-0.5)
    corr = (
        lax.dot_general(queries, keys, (((1,), (1,)), ((), ())), preferred_element_type=jnp.float32)
        * scale
    ).astype(jnp.bfloat16)

    offsets = blk_offset[0, 0]
    classes = blk_class[0, 0]
    live = blk_count[0, 0]
    slots = offsets.shape[0]
    used = (jnp.arange(slots, dtype=jnp.int32) < live).astype(jnp.float32)
    by_offset = (offsets[None, :] + RMAX == jnp.arange(2 * RMAX + 1, dtype=jnp.int32)[:, None])
    by_class = classes[:, None] == jnp.arange(NCLASS, dtype=jnp.int32)[None, :]
    counts = jnp.dot(
        by_offset.astype(jnp.float32) * used[None, :],
        by_class.astype(jnp.float32),
        precision=lax.Precision.HIGHEST,
    )
    weight = jnp.einsum(
        "oc,cph->oph",
        counts.astype(jnp.bfloat16),
        corr_proj,
        preferred_element_type=jnp.float32,
    ).reshape((2 * RMAX + 1) * points, hid)
    weight_hi = weight.astype(jnp.bfloat16)
    weight_lo = (weight - weight_hi.astype(jnp.float32)).astype(jnp.bfloat16)
    both = jnp.dot(
        corr, jnp.concatenate([weight_hi, weight_lo], axis=1), preferred_element_type=jnp.float32
    )
    motion_sum = both[:, :hid] + both[:, hid:]
    motion = jnp.maximum(motion_sum, 0.0).astype(jnp.bfloat16).reshape(rows, cols, hid)
    joined = jnp.concatenate([context_in, motion], axis=2)
    x_lon = valid_conv(
        rim_lon(joined.transpose(1, 0, 2), HALO), input_conv[0], cols + 2 * (HALO - 2)
    )
    x_lat = valid_conv(rim_lat(joined, HALO), input_conv[1], rows + 2 * (HALO - 2))
    state = hidden_init.astype(jnp.float32)
    for step in range(ITERS):
        state = gru_pass(
            state.transpose(1, 0, 2),
            x_lon,
            rim_lon,
            state_zr[0],
            state_q[0],
            update_bias[0],
            gate_bias[0],
        ).transpose(1, 0, 2)
        state = gru_pass(
            state, x_lat, rim_lat, state_zr[1], state_q[1], update_bias[1], gate_bias[1]
        )
    return state.astype(jnp.bfloat16)


def solution(mesh):
    placed = (
        P("lat", "lon", None),
        P("lat", "lon", None),
        P("lat", "lon", None),
        P("lat", "lon", None),
        P(),
        P(),
        P(),
        P(),
        P(),
        P(),
        P("lat", "lon", None),
        P("lat", "lon", None),
        P("lat", "lon"),
    )
    return jax.shard_map(
        local, mesh=mesh, in_specs=placed, out_specs=P("lat", "lon", None), check_vma=False
    )
```

```python
import jax
import jax.numpy as jnp
from jax import lax
from jax.sharding import PartitionSpec as P

POOLR = 8
POOLC = 16
RMAX = 4
ITERS = 4
NCLASS = 8
HALO = 4


def passed_along(value, axis, steps):
    count = lax.axis_size(axis)
    pairs = [(source, (source + steps) % count) for source in range(count)]
    return lax.ppermute(value, axis, pairs)


def swap_lon(values, width):
    count = lax.axis_size("lon")
    forward = [(i, (i + 1) % count) for i in range(count)]
    backward = [(target, source) for source, target in forward]
    low = lax.ppermute(values[values.shape[0] - width :], "lon", forward)
    high = lax.ppermute(values[:width], "lon", backward)
    return low, high


def swap_lat(values, width):
    count = lax.axis_size("lat")
    here = lax.axis_index("lat")
    forward = [(i, (i + 1) % count) for i in range(count)]
    backward = [(target, source) for source, target in forward]
    low = lax.ppermute(values[values.shape[0] - width :], "lat", forward)
    high = lax.ppermute(values[:width], "lat", backward)
    low = jnp.where(here > 0, low, jnp.zeros_like(low))
    high = jnp.where(here < count - 1, high, jnp.zeros_like(high))
    return low, high


def split_pair(values):
    high = values.astype(jnp.bfloat16)
    rest = (values - high.astype(jnp.float32)).astype(jnp.bfloat16)
    return jnp.concatenate([high, rest], axis=-1)


def edges(values, width):
    return jnp.concatenate([values[:width], values[values.shape[0] - width :]], axis=0)


def swap_state(state, swap):
    low, high = swap(split_pair(edges(state, HALO)), HALO)
    return low, high


def valid_conv(padded, weight, out_len):
    other = padded.shape[1]
    total = None
    for tap in range(5):
        piece = padded[tap : tap + out_len].reshape(-1, padded.shape[2])
        term = jnp.dot(piece, weight[tap], preferred_element_type=jnp.float32)
        total = term if total is None else total + term
    return total.reshape(out_len, other, -1)


def gru_pass(state, low, high, inputs, zr_weight, q_weight, z_bias, gate_row):
    hid = state.shape[2]
    size = state.shape[0]
    inner = size + 2 * (HALO - 2)
    wide_bf = jnp.concatenate(
        [low[..., :hid], state.astype(jnp.bfloat16), high[..., :hid]], axis=0
    )
    low_f = low[..., :hid].astype(jnp.float32) + low[..., hid:].astype(jnp.float32)
    high_f = high[..., :hid].astype(jnp.float32) + high[..., hid:].astype(jnp.float32)
    mid = jnp.concatenate([low_f[2:], state, high_f[: HALO - 2]], axis=0)
    mixed = valid_conv(wide_bf, zr_weight, inner)
    reset = jax.nn.sigmoid(inputs[..., hid : 2 * hid] + mixed[..., hid:] + gate_row[:hid])
    reset_state = (reset * mid).astype(jnp.bfloat16)
    core_x = inputs[HALO - 2 : HALO - 2 + size]
    core_mixed = mixed[HALO - 2 : HALO - 2 + size]
    update = jax.nn.sigmoid(core_x[..., :hid] + core_mixed[..., :hid] + z_bias)
    candidate = jnp.tanh(
        core_x[..., 2 * hid :] + valid_conv(reset_state, q_weight, size) + gate_row[hid:]
    )
    return (1.0 - update) * state + update * candidate


def local(
    feat_one,
    feat_two,
    context_in,
    hidden_init,
    corr_proj,
    input_conv,
    state_zr,
    state_q,
    update_bias,
    gate_bias,
    blk_offset,
    blk_class,
    blk_count,
):
    rows, cols, chans = feat_one.shape
    hid = hidden_init.shape[2]
    pool_rows = rows // POOLR
    pool_cols = cols // POOLC
    points = POOLR * POOLC
    cell = jnp.arange(rows * cols, dtype=jnp.int32)
    window = (cell // (cols * pool_rows)) * POOLC + (cell % cols) // pool_cols
    pool_mat = jnp.where(
        window[None, :] == jnp.arange(points, dtype=jnp.int32)[:, None],
        jnp.bfloat16(1.0 / (pool_rows * pool_cols)),
        jnp.bfloat16(0.0),
    )
    pooled = jnp.dot(
        pool_mat, feat_two.reshape(rows * cols, chans), preferred_element_type=jnp.float32
    ).astype(jnp.bfloat16)
    near = jnp.concatenate(
        [passed_along(pooled, "lon", 1), pooled, passed_along(pooled, "lon", -1)], axis=0
    )
    reach = 3
    keys = jnp.concatenate(
        [passed_along(near, "lon", reach), near, passed_along(near, "lon", -reach)], axis=0
    )

    queries = feat_one.reshape(rows * cols, chans)
    scale = chans ** (-0.5)
    corr = (
        lax.dot_general(queries, keys, (((1,), (1,)), ((), ())), preferred_element_type=jnp.float32)
        * scale
    ).astype(jnp.bfloat16)

    offsets = blk_offset[0, 0]
    classes = blk_class[0, 0]
    live = blk_count[0, 0]
    slots = offsets.shape[0]
    used = (jnp.arange(slots, dtype=jnp.int32) < live).astype(jnp.float32)
    by_offset = (offsets[None, :] + RMAX == jnp.arange(2 * RMAX + 1, dtype=jnp.int32)[:, None])
    by_class = classes[:, None] == jnp.arange(NCLASS, dtype=jnp.int32)[None, :]
    counts = jnp.dot(
        by_offset.astype(jnp.float32) * used[None, :],
        by_class.astype(jnp.float32),
        precision=lax.Precision.HIGHEST,
    )
    weight = jnp.einsum(
        "oc,cph->oph",
        counts.astype(jnp.bfloat16),
        corr_proj,
        preferred_element_type=jnp.float32,
    ).reshape((2 * RMAX + 1) * points, hid)
    weight_hi = weight.astype(jnp.bfloat16)
    weight_lo = (weight - weight_hi.astype(jnp.float32)).astype(jnp.bfloat16)
    both = jnp.dot(
        corr, jnp.concatenate([weight_hi, weight_lo], axis=1), preferred_element_type=jnp.float32
    )
    motion_sum = both[:, :hid] + both[:, hid:]
    motion = jnp.maximum(motion_sum, 0.0).astype(jnp.bfloat16).reshape(rows, cols, hid)
    joined = jnp.concatenate([context_in, motion], axis=2)
    chan_in = joined.shape[2]
    joined_t = joined.transpose(1, 0, 2)
    hidden_t = hidden_init.transpose(1, 0, 2)
    low, high = swap_lon(jnp.concatenate([joined_t, hidden_t], axis=2), HALO)
    x_lon = valid_conv(
        jnp.concatenate([low[..., :chan_in], joined_t, high[..., :chan_in]], axis=0),
        input_conv[0],
        cols + 2 * (HALO - 2),
    )
    nothing = jnp.zeros_like(low[..., chan_in:])
    state_low = jnp.concatenate([low[..., chan_in:], nothing], axis=2)
    state_high = jnp.concatenate([high[..., chan_in:], nothing], axis=2)
    state = hidden_t.astype(jnp.float32)
    x_lat = None
    for step in range(ITERS):
        state = gru_pass(
            state, state_low, state_high, x_lon, state_zr[0], state_q[0], update_bias[0], gate_bias[0]
        ).transpose(1, 0, 2)
        if x_lat is None:
            sent = jnp.concatenate([edges(joined, HALO), split_pair(edges(state, HALO))], axis=2)
            low, high = swap_lat(sent, HALO)
            x_lat = valid_conv(
                jnp.concatenate([low[..., :chan_in], joined, high[..., :chan_in]], axis=0),
                input_conv[1],
                rows + 2 * (HALO - 2),
            )
            state_low, state_high = low[..., chan_in:], high[..., chan_in:]
        else:
            state_low, state_high = swap_state(state, swap_lat)
        state = gru_pass(
            state, state_low, state_high, x_lat, state_zr[1], state_q[1], update_bias[1], gate_bias[1]
        )
        if step < ITERS - 1:
            state = state.transpose(1, 0, 2)
            state_low, state_high = swap_state(state, swap_lon)
    return state.astype(jnp.bfloat16)


def solution(mesh):
    placed = (
        P("lat", "lon", None),
        P("lat", "lon", None),
        P("lat", "lon", None),
        P("lat", "lon", None),
        P(),
        P(),
        P(),
        P(),
        P(),
        P(),
        P("lat", "lon", None),
        P("lat", "lon", None),
        P("lat", "lon"),
    )
    return jax.shard_map(
        local, mesh=mesh, in_specs=placed, out_specs=P("lat", "lon", None), check_vma=False
    )
```

```python
import jax
import jax.numpy as jnp
from jax import lax
from jax.experimental import pallas as pl
from jax.experimental.pallas import tpu as pltpu
from jax.sharding import PartitionSpec as P

POOLR = 8
POOLC = 16
RMAX = 4
ITERS = 4
NCLASS = 8
HALO = 4


def passed_along(value, axis, steps):
    count = lax.axis_size(axis)
    pairs = [(source, (source + steps) % count) for source in range(count)]
    return lax.ppermute(value, axis, pairs)


def swap_lon(values, width):
    count = lax.axis_size("lon")
    forward = [(i, (i + 1) % count) for i in range(count)]
    backward = [(target, source) for source, target in forward]
    low = lax.ppermute(values[values.shape[0] - width :], "lon", forward)
    high = lax.ppermute(values[:width], "lon", backward)
    return low, high


def swap_lat(values, width):
    count = lax.axis_size("lat")
    here = lax.axis_index("lat")
    forward = [(i, (i + 1) % count) for i in range(count)]
    backward = [(target, source) for source, target in forward]
    low = lax.ppermute(values[values.shape[0] - width :], "lat", forward)
    high = lax.ppermute(values[:width], "lat", backward)
    low = jnp.where(here > 0, low, jnp.zeros_like(low))
    high = jnp.where(here < count - 1, high, jnp.zeros_like(high))
    return low, high


def split_pair(values):
    high = values.astype(jnp.bfloat16)
    rest = (values - high.astype(jnp.float32)).astype(jnp.bfloat16)
    return jnp.concatenate([high, rest], axis=-1)


def edges(values, width):
    return jnp.concatenate([values[:width], values[values.shape[0] - width :]], axis=0)


def swap_state(state, swap):
    low, high = swap(split_pair(edges(state, HALO)), HALO)
    return low, high


def valid_conv(padded, weight, out_len):
    other = padded.shape[1]
    total = None
    for tap in range(5):
        piece = padded[tap : tap + out_len].reshape(-1, padded.shape[2])
        term = jnp.dot(piece, weight[tap], preferred_element_type=jnp.float32)
        total = term if total is None else total + term
    return total.reshape(out_len, other, -1)


def gru_kernel(
    state_ref, low_ref, high_ref, x_ref, zr_ref, q_ref, zb_ref, gr_ref, out_ref, wide, mid, reset_state
):
    hid = state_ref.shape[1]
    line = low_ref.shape[0] // HALO
    total = state_ref.shape[0]
    inner = total + 2 * (HALO - 2) * line
    state = state_ref[...]
    wide[: HALO * line] = low_ref[:, :hid]
    wide[HALO * line : HALO * line + total] = state.astype(jnp.bfloat16)
    wide[HALO * line + total :] = high_ref[:, :hid]
    side = (HALO - 2) * line
    mid[:side] = (
        low_ref[2 * line :, :hid].astype(jnp.float32) + low_ref[2 * line :, hid:].astype(jnp.float32)
    )
    mid[side : side + total] = state
    mid[side + total :] = (
        high_ref[:side, :hid].astype(jnp.float32) + high_ref[:side, hid:].astype(jnp.float32)
    )
    mixed = None
    for tap in range(5):
        term = jnp.dot(
            wide[tap * line : tap * line + inner], zr_ref[tap], preferred_element_type=jnp.float32
        )
        mixed = term if mixed is None else mixed + term
    gate_row = gr_ref[...]
    reset = jax.nn.sigmoid(x_ref[:, hid : 2 * hid] + mixed[:, hid:] + gate_row[:, :hid])
    reset_state[...] = (reset * mid[...]).astype(jnp.bfloat16)
    cand = None
    for tap in range(5):
        term = jnp.dot(
            reset_state[tap * line : tap * line + total],
            q_ref[tap],
            preferred_element_type=jnp.float32,
        )
        cand = term if cand is None else cand + term
    core_x = x_ref[side : side + total]
    update = jax.nn.sigmoid(core_x[:, :hid] + mixed[side : side + total, :hid] + zb_ref[...])
    candidate = jnp.tanh(core_x[:, 2 * hid :] + cand + gate_row[:, hid:])
    out_ref[...] = (1.0 - update) * state + update * candidate


def gru_pass(state, low, high, inputs, zr_weight, q_weight, z_bias, gate_row):
    size, line, hid = state.shape
    total = size * line
    inner = total + 2 * (HALO - 2) * line
    vmem = pl.BlockSpec(memory_space=pltpu.VMEM)
    out = pl.pallas_call(
        gru_kernel,
        out_shape=jax.ShapeDtypeStruct((total, hid), jnp.float32),
        in_specs=[vmem] * 8,
        out_specs=vmem,
        scratch_shapes=[
            pltpu.VMEM((total + 2 * HALO * line, hid), jnp.bfloat16),
            pltpu.VMEM((inner, hid), jnp.float32),
            pltpu.VMEM((inner, hid), jnp.bfloat16),
        ],
        cost_estimate=pl.CostEstimate(
            flops=2 * 5 * hid * (inner * 2 * hid + total * hid),
            transcendentals=inner * hid + 2 * total * hid,
            bytes_accessed=4 * (2 * total * hid + inner * 3 * hid),
        ),
    )(
        state.reshape(total, hid),
        low.reshape(HALO * line, 2 * hid),
        high.reshape(HALO * line, 2 * hid),
        inputs.reshape(inner, 3 * hid),
        zr_weight,
        q_weight,
        z_bias.reshape(1, hid),
        gate_row.reshape(1, 2 * hid),
    )
    return out.reshape(size, line, hid)


def local(
    feat_one,
    feat_two,
    context_in,
    hidden_init,
    corr_proj,
    input_conv,
    state_zr,
    state_q,
    update_bias,
    gate_bias,
    blk_offset,
    blk_class,
    blk_count,
):
    rows, cols, chans = feat_one.shape
    hid = hidden_init.shape[2]
    pool_rows = rows // POOLR
    pool_cols = cols // POOLC
    points = POOLR * POOLC
    cell = jnp.arange(rows * cols, dtype=jnp.int32)
    window = (cell // (cols * pool_rows)) * POOLC + (cell % cols) // pool_cols
    pool_mat = jnp.where(
        window[None, :] == jnp.arange(points, dtype=jnp.int32)[:, None],
        jnp.bfloat16(1.0 / (pool_rows * pool_cols)),
        jnp.bfloat16(0.0),
    )
    pooled = jnp.dot(
        pool_mat, feat_two.reshape(rows * cols, chans), preferred_element_type=jnp.float32
    ).astype(jnp.bfloat16)
    near = jnp.concatenate(
        [passed_along(pooled, "lon", 1), pooled, passed_along(pooled, "lon", -1)], axis=0
    )
    reach = 3
    keys = jnp.concatenate(
        [passed_along(near, "lon", reach), near, passed_along(near, "lon", -reach)], axis=0
    )

    queries = feat_one.reshape(rows * cols, chans)
    scale = chans ** (-0.5)
    corr = (
        lax.dot_general(queries, keys, (((1,), (1,)), ((), ())), preferred_element_type=jnp.float32)
        * scale
    ).astype(jnp.bfloat16)

    offsets = blk_offset[0, 0]
    classes = blk_class[0, 0]
    live = blk_count[0, 0]
    slots = offsets.shape[0]
    used = (jnp.arange(slots, dtype=jnp.int32) < live).astype(jnp.float32)
    by_offset = (offsets[None, :] + RMAX == jnp.arange(2 * RMAX + 1, dtype=jnp.int32)[:, None])
    by_class = classes[:, None] == jnp.arange(NCLASS, dtype=jnp.int32)[None, :]
    counts = jnp.dot(
        by_offset.astype(jnp.float32) * used[None, :],
        by_class.astype(jnp.float32),
        precision=lax.Precision.HIGHEST,
    )
    weight = jnp.einsum(
        "oc,cph->oph",
        counts.astype(jnp.bfloat16),
        corr_proj,
        preferred_element_type=jnp.float32,
    ).reshape((2 * RMAX + 1) * points, hid)
    weight_hi = weight.astype(jnp.bfloat16)
    weight_lo = (weight - weight_hi.astype(jnp.float32)).astype(jnp.bfloat16)
    both = jnp.dot(
        corr, jnp.concatenate([weight_hi, weight_lo], axis=1), preferred_element_type=jnp.float32
    )
    motion_sum = both[:, :hid] + both[:, hid:]
    motion = jnp.maximum(motion_sum, 0.0).astype(jnp.bfloat16).reshape(rows, cols, hid)
    joined = jnp.concatenate([context_in, motion], axis=2)
    chan_in = joined.shape[2]
    joined_t = joined.transpose(1, 0, 2)
    hidden_t = hidden_init.transpose(1, 0, 2)
    low, high = swap_lon(jnp.concatenate([joined_t, hidden_t], axis=2), HALO)
    x_lon = valid_conv(
        jnp.concatenate([low[..., :chan_in], joined_t, high[..., :chan_in]], axis=0),
        input_conv[0],
        cols + 2 * (HALO - 2),
    )
    nothing = jnp.zeros_like(low[..., chan_in:])
    state_low = jnp.concatenate([low[..., chan_in:], nothing], axis=2)
    state_high = jnp.concatenate([high[..., chan_in:], nothing], axis=2)
    state = hidden_t.astype(jnp.float32)
    x_lat = None
    for step in range(ITERS):
        state = gru_pass(
            state, state_low, state_high, x_lon, state_zr[0], state_q[0], update_bias[0], gate_bias[0]
        ).transpose(1, 0, 2)
        if x_lat is None:
            sent = jnp.concatenate([edges(joined, HALO), split_pair(edges(state, HALO))], axis=2)
            low, high = swap_lat(sent, HALO)
            x_lat = valid_conv(
                jnp.concatenate([low[..., :chan_in], joined, high[..., :chan_in]], axis=0),
                input_conv[1],
                rows + 2 * (HALO - 2),
            )
            state_low, state_high = low[..., chan_in:], high[..., chan_in:]
        else:
            state_low, state_high = swap_state(state, swap_lat)
        state = gru_pass(
            state, state_low, state_high, x_lat, state_zr[1], state_q[1], update_bias[1], gate_bias[1]
        )
        if step < ITERS - 1:
            state = state.transpose(1, 0, 2)
            state_low, state_high = swap_state(state, swap_lon)
    return state.astype(jnp.bfloat16)


def solution(mesh):
    placed = (
        P("lat", "lon", None),
        P("lat", "lon", None),
        P("lat", "lon", None),
        P("lat", "lon", None),
        P(),
        P(),
        P(),
        P(),
        P(),
        P(),
        P("lat", "lon", None),
        P("lat", "lon", None),
        P("lat", "lon"),
    )
    return jax.shard_map(
        local, mesh=mesh, in_specs=placed, out_specs=P("lat", "lon", None), check_vma=False
    )
```

```python
import jax
import jax.numpy as jnp
from jax import lax
from jax.experimental import pallas as pl
from jax.experimental.pallas import tpu as pltpu
from jax.sharding import PartitionSpec as P

POOLR = 8
POOLC = 16
RMAX = 4
ITERS = 4
NCLASS = 8
HALO = 4


def passed_along(value, axis, steps):
    count = lax.axis_size(axis)
    pairs = [(source, (source + steps) % count) for source in range(count)]
    return lax.ppermute(value, axis, pairs)


def swap_lon(values, width):
    count = lax.axis_size("lon")
    forward = [(i, (i + 1) % count) for i in range(count)]
    backward = [(target, source) for source, target in forward]
    low = lax.ppermute(values[values.shape[0] - width :], "lon", forward)
    high = lax.ppermute(values[:width], "lon", backward)
    return low, high


def swap_lat(values, width):
    count = lax.axis_size("lat")
    here = lax.axis_index("lat")
    forward = [(i, (i + 1) % count) for i in range(count)]
    backward = [(target, source) for source, target in forward]
    low = lax.ppermute(values[values.shape[0] - width :], "lat", forward)
    high = lax.ppermute(values[:width], "lat", backward)
    low = jnp.where(here > 0, low, jnp.zeros_like(low))
    high = jnp.where(here < count - 1, high, jnp.zeros_like(high))
    return low, high


def split_pair(values):
    high = values.astype(jnp.bfloat16)
    rest = (values - high.astype(jnp.float32)).astype(jnp.bfloat16)
    return jnp.concatenate([high, rest], axis=-1)


def edges(values, width):
    return jnp.concatenate([values[:width], values[values.shape[0] - width :]], axis=0)


def swap_state(state, swap):
    low, high = swap(split_pair(edges(state, HALO)), HALO)
    return low, high


def valid_conv(padded, weight, out_len):
    other = padded.shape[1]
    total = None
    for tap in range(5):
        piece = padded[tap : tap + out_len].reshape(-1, padded.shape[2])
        term = jnp.dot(piece, weight[tap], preferred_element_type=jnp.float32)
        total = term if total is None else total + term
    return total.reshape(out_len, other, -1)


def gru_kernel(
    state_ref,
    low_ref,
    high_ref,
    x_ref,
    zr_ref,
    q_ref,
    zb_ref,
    gr_ref,
    out_ref,
    wide,
    mid,
    reset_state,
    taps,
    reset_taps,
):
    hid = state_ref.shape[1]
    line = low_ref.shape[0] // HALO
    total = state_ref.shape[0]
    inner = total + 2 * (HALO - 2) * line
    state = state_ref[...]
    wide[: HALO * line] = low_ref[:, :hid]
    wide[HALO * line : HALO * line + total] = state.astype(jnp.bfloat16)
    wide[HALO * line + total :] = high_ref[:, :hid]
    side = (HALO - 2) * line
    mid[:side] = (
        low_ref[2 * line :, :hid].astype(jnp.float32) + low_ref[2 * line :, hid:].astype(jnp.float32)
    )
    mid[side : side + total] = state
    mid[side + total :] = (
        high_ref[:side, :hid].astype(jnp.float32) + high_ref[:side, hid:].astype(jnp.float32)
    )
    for tap in range(5):
        taps[:, tap * hid : (tap + 1) * hid] = wide[tap * line : tap * line + inner]
    mixed = jnp.dot(taps[...], zr_ref[...], preferred_element_type=jnp.float32)
    gate_row = gr_ref[...]
    reset = jax.nn.sigmoid(x_ref[:, hid : 2 * hid] + mixed[:, hid:] + gate_row[:, :hid])
    reset_state[...] = (reset * mid[...]).astype(jnp.bfloat16)
    for tap in range(5):
        reset_taps[:, tap * hid : (tap + 1) * hid] = reset_state[tap * line : tap * line + total]
    cand = jnp.dot(reset_taps[...], q_ref[...], preferred_element_type=jnp.float32)
    core_x = x_ref[side : side + total]
    update = jax.nn.sigmoid(core_x[:, :hid] + mixed[side : side + total, :hid] + zb_ref[...])
    candidate = jnp.tanh(core_x[:, 2 * hid :] + cand + gate_row[:, hid:])
    out_ref[...] = (1.0 - update) * state + update * candidate


def gru_pass(state, low, high, inputs, zr_weight, q_weight, z_bias, gate_row):
    size, line, hid = state.shape
    total = size * line
    inner = total + 2 * (HALO - 2) * line
    vmem = pl.BlockSpec(memory_space=pltpu.VMEM)
    out = pl.pallas_call(
        gru_kernel,
        out_shape=jax.ShapeDtypeStruct((total, hid), jnp.float32),
        in_specs=[vmem] * 8,
        out_specs=vmem,
        scratch_shapes=[
            pltpu.VMEM((total + 2 * HALO * line, hid), jnp.bfloat16),
            pltpu.VMEM((inner, hid), jnp.float32),
            pltpu.VMEM((inner, hid), jnp.bfloat16),
            pltpu.VMEM((inner, 5 * hid), jnp.bfloat16),
            pltpu.VMEM((total, 5 * hid), jnp.bfloat16),
        ],
        cost_estimate=pl.CostEstimate(
            flops=2 * 5 * hid * (inner * 2 * hid + total * hid),
            transcendentals=inner * hid + 2 * total * hid,
            bytes_accessed=4 * (2 * total * hid + inner * 3 * hid),
        ),
    )(
        state.reshape(total, hid),
        low.reshape(HALO * line, 2 * hid),
        high.reshape(HALO * line, 2 * hid),
        inputs.reshape(inner, 3 * hid),
        zr_weight.reshape(5 * hid, 2 * hid),
        q_weight.reshape(5 * hid, hid),
        z_bias.reshape(1, hid),
        gate_row.reshape(1, 2 * hid),
    )
    return out.reshape(size, line, hid)


def local(
    feat_one,
    feat_two,
    context_in,
    hidden_init,
    corr_proj,
    input_conv,
    state_zr,
    state_q,
    update_bias,
    gate_bias,
    blk_offset,
    blk_class,
    blk_count,
):
    rows, cols, chans = feat_one.shape
    hid = hidden_init.shape[2]
    pool_rows = rows // POOLR
    pool_cols = cols // POOLC
    points = POOLR * POOLC
    cell = jnp.arange(rows * cols, dtype=jnp.int32)
    window = (cell // (cols * pool_rows)) * POOLC + (cell % cols) // pool_cols
    pool_mat = jnp.where(
        window[None, :] == jnp.arange(points, dtype=jnp.int32)[:, None],
        jnp.bfloat16(1.0 / (pool_rows * pool_cols)),
        jnp.bfloat16(0.0),
    )
    pooled = jnp.dot(
        pool_mat, feat_two.reshape(rows * cols, chans), preferred_element_type=jnp.float32
    ).astype(jnp.bfloat16)
    near = jnp.concatenate(
        [passed_along(pooled, "lon", 1), pooled, passed_along(pooled, "lon", -1)], axis=0
    )
    reach = 3
    keys = jnp.concatenate(
        [passed_along(near, "lon", reach), near, passed_along(near, "lon", -reach)], axis=0
    )

    queries = feat_one.reshape(rows * cols, chans)
    scale = chans ** (-0.5)
    corr = (
        lax.dot_general(queries, keys, (((1,), (1,)), ((), ())), preferred_element_type=jnp.float32)
        * scale
    ).astype(jnp.bfloat16)

    offsets = blk_offset[0, 0]
    classes = blk_class[0, 0]
    live = blk_count[0, 0]
    slots = offsets.shape[0]
    used = (jnp.arange(slots, dtype=jnp.int32) < live).astype(jnp.float32)
    by_offset = (offsets[None, :] + RMAX == jnp.arange(2 * RMAX + 1, dtype=jnp.int32)[:, None])
    by_class = classes[:, None] == jnp.arange(NCLASS, dtype=jnp.int32)[None, :]
    counts = jnp.dot(
        by_offset.astype(jnp.float32) * used[None, :],
        by_class.astype(jnp.float32),
        precision=lax.Precision.HIGHEST,
    )
    weight = jnp.einsum(
        "oc,cph->oph",
        counts.astype(jnp.bfloat16),
        corr_proj,
        preferred_element_type=jnp.float32,
    ).reshape((2 * RMAX + 1) * points, hid)
    weight_hi = weight.astype(jnp.bfloat16)
    weight_lo = (weight - weight_hi.astype(jnp.float32)).astype(jnp.bfloat16)
    both = jnp.dot(
        corr, jnp.concatenate([weight_hi, weight_lo], axis=1), preferred_element_type=jnp.float32
    )
    motion_sum = both[:, :hid] + both[:, hid:]
    motion = jnp.maximum(motion_sum, 0.0).astype(jnp.bfloat16).reshape(rows, cols, hid)
    joined = jnp.concatenate([context_in, motion], axis=2)
    chan_in = joined.shape[2]
    joined_t = joined.transpose(1, 0, 2)
    hidden_t = hidden_init.transpose(1, 0, 2)
    low, high = swap_lon(jnp.concatenate([joined_t, hidden_t], axis=2), HALO)
    x_lon = valid_conv(
        jnp.concatenate([low[..., :chan_in], joined_t, high[..., :chan_in]], axis=0),
        input_conv[0],
        cols + 2 * (HALO - 2),
    )
    nothing = jnp.zeros_like(low[..., chan_in:])
    state_low = jnp.concatenate([low[..., chan_in:], nothing], axis=2)
    state_high = jnp.concatenate([high[..., chan_in:], nothing], axis=2)
    state = hidden_t.astype(jnp.float32)
    x_lat = None
    for step in range(ITERS):
        state = gru_pass(
            state, state_low, state_high, x_lon, state_zr[0], state_q[0], update_bias[0], gate_bias[0]
        ).transpose(1, 0, 2)
        if x_lat is None:
            sent = jnp.concatenate([edges(joined, HALO), split_pair(edges(state, HALO))], axis=2)
            low, high = swap_lat(sent, HALO)
            x_lat = valid_conv(
                jnp.concatenate([low[..., :chan_in], joined, high[..., :chan_in]], axis=0),
                input_conv[1],
                rows + 2 * (HALO - 2),
            )
            state_low, state_high = low[..., chan_in:], high[..., chan_in:]
        else:
            state_low, state_high = swap_state(state, swap_lat)
        state = gru_pass(
            state, state_low, state_high, x_lat, state_zr[1], state_q[1], update_bias[1], gate_bias[1]
        )
        if step < ITERS - 1:
            state = state.transpose(1, 0, 2)
            state_low, state_high = swap_state(state, swap_lon)
    return state.astype(jnp.bfloat16)


def solution(mesh):
    placed = (
        P("lat", "lon", None),
        P("lat", "lon", None),
        P("lat", "lon", None),
        P("lat", "lon", None),
        P(),
        P(),
        P(),
        P(),
        P(),
        P(),
        P("lat", "lon", None),
        P("lat", "lon", None),
        P("lat", "lon"),
    )
    return jax.shard_map(
        local, mesh=mesh, in_specs=placed, out_specs=P("lat", "lon", None), check_vma=False
    )
```

```python
import functools

import jax
import jax.numpy as jnp
from jax import lax
from jax.experimental import pallas as pl
from jax.experimental.pallas import tpu as pltpu
from jax.sharding import PartitionSpec as P

POOLR = 8
POOLC = 16
RMAX = 4
ITERS = 4
NCLASS = 8
HALO = 4


def passed_along(value, axis, steps):
    count = lax.axis_size(axis)
    pairs = [(source, (source + steps) % count) for source in range(count)]
    return lax.ppermute(value, axis, pairs)


def swap_lon(values, width):
    count = lax.axis_size("lon")
    forward = [(i, (i + 1) % count) for i in range(count)]
    backward = [(target, source) for source, target in forward]
    low = lax.ppermute(values[values.shape[0] - width :], "lon", forward)
    high = lax.ppermute(values[:width], "lon", backward)
    return low, high


def swap_lat(values, width):
    count = lax.axis_size("lat")
    here = lax.axis_index("lat")
    forward = [(i, (i + 1) % count) for i in range(count)]
    backward = [(target, source) for source, target in forward]
    last = values[values.shape[0] - width :]
    first = values[:width]
    last = jnp.where(here < count - 1, last, jnp.zeros_like(last))
    first = jnp.where(here > 0, first, jnp.zeros_like(first))
    low = lax.ppermute(last, "lat", forward)
    high = lax.ppermute(first, "lat", backward)
    return low, high


def split_pair(values):
    high = values.astype(jnp.bfloat16)
    rest = (values - high.astype(jnp.float32)).astype(jnp.bfloat16)
    return jnp.concatenate([high, rest], axis=-1)


def edges(values, width):
    return jnp.concatenate([values[:width], values[values.shape[0] - width :]], axis=0)


def swap_state(state, swap):
    low, high = swap(split_pair(edges(state, HALO)), HALO)
    return low, high


def valid_conv(padded, weight, out_len):
    other = padded.shape[1]
    total = None
    for tap in range(5):
        piece = padded[tap : tap + out_len].reshape(-1, padded.shape[2])
        term = jnp.dot(piece, weight[tap], preferred_element_type=jnp.float32)
        total = term if total is None else total + term
    return total.reshape(out_len, other, -1)


def gru_kernel(
    flip,
    state_ref,
    low_ref,
    high_ref,
    x_ref,
    zr_ref,
    q_ref,
    zb_ref,
    gr_ref,
    out_ref,
    wide,
    mid,
    reset_state,
    taps,
    reset_taps,
):
    hid = state_ref.shape[1]
    line = low_ref.shape[0] // HALO
    total = state_ref.shape[0]
    inner = total + 2 * (HALO - 2) * line
    state = state_ref[...]
    wide[: HALO * line] = low_ref[:, :hid]
    wide[HALO * line : HALO * line + total] = state.astype(jnp.bfloat16)
    wide[HALO * line + total :] = high_ref[:, :hid]
    side = (HALO - 2) * line
    mid[:side] = (
        low_ref[2 * line :, :hid].astype(jnp.float32) + low_ref[2 * line :, hid:].astype(jnp.float32)
    )
    mid[side : side + total] = state
    mid[side + total :] = (
        high_ref[:side, :hid].astype(jnp.float32) + high_ref[:side, hid:].astype(jnp.float32)
    )
    for tap in range(5):
        taps[:, tap * hid : (tap + 1) * hid] = wide[tap * line : tap * line + inner]
    mixed = jnp.dot(taps[...], zr_ref[...], preferred_element_type=jnp.float32)
    gate_row = gr_ref[...]
    reset = jax.nn.sigmoid(x_ref[:, hid : 2 * hid] + mixed[:, hid:] + gate_row[:, :hid])
    reset_state[...] = (reset * mid[...]).astype(jnp.bfloat16)
    for tap in range(5):
        reset_taps[:, tap * hid : (tap + 1) * hid] = reset_state[tap * line : tap * line + total]
    cand = jnp.dot(reset_taps[...], q_ref[...], preferred_element_type=jnp.float32)
    core_x = x_ref[side : side + total]
    update = jax.nn.sigmoid(core_x[:, :hid] + mixed[side : side + total, :hid] + zb_ref[...])
    candidate = jnp.tanh(core_x[:, 2 * hid :] + cand + gate_row[:, hid:])
    new = (1.0 - update) * state + update * candidate
    if out_ref.shape == state_ref.shape and not flip:
        out_ref[...] = new
    else:
        size = total // line
        for a in range(size):
            out_ref[pl.ds(a, line, stride=size)] = new[a * line : (a + 1) * line]


def gru_pass(state, low, high, inputs, zr_weight, q_weight, z_bias, gate_row, flip=True):
    size, line, hid = state.shape
    total = size * line
    inner = total + 2 * (HALO - 2) * line
    vmem = pl.BlockSpec(memory_space=pltpu.VMEM)
    out = pl.pallas_call(
        functools.partial(gru_kernel, flip),
        out_shape=jax.ShapeDtypeStruct((total, hid), jnp.float32),
        in_specs=[vmem] * 8,
        out_specs=vmem,
        scratch_shapes=[
            pltpu.VMEM((total + 2 * HALO * line, hid), jnp.bfloat16),
            pltpu.VMEM((inner, hid), jnp.float32),
            pltpu.VMEM((inner, hid), jnp.bfloat16),
            pltpu.VMEM((inner, 5 * hid), jnp.bfloat16),
            pltpu.VMEM((total, 5 * hid), jnp.bfloat16),
        ],
        cost_estimate=pl.CostEstimate(
            flops=2 * 5 * hid * (inner * 2 * hid + total * hid),
            transcendentals=inner * hid + 2 * total * hid,
            bytes_accessed=4 * (2 * total * hid + inner * 3 * hid),
        ),
    )(
        state.reshape(total, hid),
        low.reshape(HALO * line, 2 * hid),
        high.reshape(HALO * line, 2 * hid),
        inputs.reshape(inner, 3 * hid),
        zr_weight.reshape(5 * hid, 2 * hid),
        q_weight.reshape(5 * hid, hid),
        z_bias.reshape(1, hid),
        gate_row.reshape(1, 2 * hid),
    )
    if flip:
        return out.reshape(line, size, hid)
    return out.reshape(size, line, hid)


def local(
    feat_one,
    feat_two,
    context_in,
    hidden_init,
    corr_proj,
    input_conv,
    state_zr,
    state_q,
    update_bias,
    gate_bias,
    blk_offset,
    blk_class,
    blk_count,
):
    rows, cols, chans = feat_one.shape
    hid = hidden_init.shape[2]
    pool_rows = rows // POOLR
    pool_cols = cols // POOLC
    points = POOLR * POOLC
    cell = jnp.arange(rows * cols, dtype=jnp.int32)
    window = (cell // (cols * pool_rows)) * POOLC + (cell % cols) // pool_cols
    pool_mat = jnp.where(
        window[None, :] == jnp.arange(points, dtype=jnp.int32)[:, None],
        jnp.bfloat16(1.0 / (pool_rows * pool_cols)),
        jnp.bfloat16(0.0),
    )
    pooled = jnp.dot(
        pool_mat, feat_two.reshape(rows * cols, chans), preferred_element_type=jnp.float32
    ).astype(jnp.bfloat16)
    near = jnp.concatenate(
        [passed_along(pooled, "lon", 1), pooled, passed_along(pooled, "lon", -1)], axis=0
    )
    reach = 3
    keys = jnp.concatenate(
        [passed_along(near, "lon", reach), near, passed_along(near, "lon", -reach)], axis=0
    )

    queries = feat_one.reshape(rows * cols, chans)
    scale = chans ** (-0.5)
    corr = (
        lax.dot_general(queries, keys, (((1,), (1,)), ((), ())), preferred_element_type=jnp.float32)
        * scale
    ).astype(jnp.bfloat16)

    offsets = blk_offset[0, 0]
    classes = blk_class[0, 0]
    live = blk_count[0, 0]
    slots = offsets.shape[0]
    used = (jnp.arange(slots, dtype=jnp.int32) < live).astype(jnp.float32)
    by_offset = (offsets[None, :] + RMAX == jnp.arange(2 * RMAX + 1, dtype=jnp.int32)[:, None])
    by_class = classes[:, None] == jnp.arange(NCLASS, dtype=jnp.int32)[None, :]
    counts = jnp.dot(
        by_offset.astype(jnp.float32) * used[None, :],
        by_class.astype(jnp.float32),
        precision=lax.Precision.HIGHEST,
    )
    weight = jnp.einsum(
        "oc,cph->oph",
        counts.astype(jnp.bfloat16),
        corr_proj,
        preferred_element_type=jnp.float32,
    ).reshape((2 * RMAX + 1) * points, hid)
    weight_hi = weight.astype(jnp.bfloat16)
    weight_lo = (weight - weight_hi.astype(jnp.float32)).astype(jnp.bfloat16)
    both = jnp.dot(
        corr, jnp.concatenate([weight_hi, weight_lo], axis=1), preferred_element_type=jnp.float32
    )
    motion_sum = both[:, :hid] + both[:, hid:]
    motion = jnp.maximum(motion_sum, 0.0).astype(jnp.bfloat16).reshape(rows, cols, hid)
    joined = jnp.concatenate([context_in, motion], axis=2)
    chan_in = joined.shape[2]
    joined_t = joined.transpose(1, 0, 2)
    hidden_t = hidden_init.transpose(1, 0, 2)
    low, high = swap_lon(jnp.concatenate([joined_t, hidden_t], axis=2), HALO)
    x_lon = valid_conv(
        jnp.concatenate([low[..., :chan_in], joined_t, high[..., :chan_in]], axis=0),
        input_conv[0],
        cols + 2 * (HALO - 2),
    )
    nothing = jnp.zeros_like(low[..., chan_in:])
    state_low = jnp.concatenate([low[..., chan_in:], nothing], axis=2)
    state_high = jnp.concatenate([high[..., chan_in:], nothing], axis=2)
    state = hidden_t.astype(jnp.float32)
    x_lat = None
    for step in range(ITERS):
        state = gru_pass(
            state, state_low, state_high, x_lon, state_zr[0], state_q[0], update_bias[0], gate_bias[0]
        )
        if x_lat is None:
            sent = jnp.concatenate([edges(joined, HALO), split_pair(edges(state, HALO))], axis=2)
            low, high = swap_lat(sent, HALO)
            x_lat = valid_conv(
                jnp.concatenate([low[..., :chan_in], joined, high[..., :chan_in]], axis=0),
                input_conv[1],
                rows + 2 * (HALO - 2),
            )
            state_low, state_high = low[..., chan_in:], high[..., chan_in:]
        else:
            state_low, state_high = swap_state(state, swap_lat)
        last = step == ITERS - 1
        state = gru_pass(
            state,
            state_low,
            state_high,
            x_lat,
            state_zr[1],
            state_q[1],
            update_bias[1],
            gate_bias[1],
            flip=not last,
        )
        if not last:
            state_low, state_high = swap_state(state, swap_lon)
    return state.astype(jnp.bfloat16)


def solution(mesh):
    placed = (
        P("lat", "lon", None),
        P("lat", "lon", None),
        P("lat", "lon", None),
        P("lat", "lon", None),
        P(),
        P(),
        P(),
        P(),
        P(),
        P(),
        P("lat", "lon", None),
        P("lat", "lon", None),
        P("lat", "lon"),
    )
    return jax.shard_map(
        local, mesh=mesh, in_specs=placed, out_specs=P("lat", "lon", None), check_vma=False
    )
```

```python
import functools

import jax
import jax.numpy as jnp
from jax import lax
from jax.experimental import pallas as pl
from jax.experimental.pallas import tpu as pltpu
from jax.sharding import PartitionSpec as P

POOLR = 8
POOLC = 16
RMAX = 4
ITERS = 4
NCLASS = 8
HALO = 4


def passed_along(value, axis, steps):
    count = lax.axis_size(axis)
    pairs = [(source, (source + steps) % count) for source in range(count)]
    return lax.ppermute(value, axis, pairs)


def swap_lon(values, width):
    count = lax.axis_size("lon")
    forward = [(i, (i + 1) % count) for i in range(count)]
    backward = [(target, source) for source, target in forward]
    low = lax.ppermute(values[values.shape[0] - width :], "lon", forward)
    high = lax.ppermute(values[:width], "lon", backward)
    return low, high


def swap_lat(values, width):
    count = lax.axis_size("lat")
    here = lax.axis_index("lat")
    forward = [(i, (i + 1) % count) for i in range(count)]
    backward = [(target, source) for source, target in forward]
    last = values[values.shape[0] - width :]
    first = values[:width]
    last = jnp.where(here < count - 1, last, jnp.zeros_like(last))
    first = jnp.where(here > 0, first, jnp.zeros_like(first))
    low = lax.ppermute(last, "lat", forward)
    high = lax.ppermute(first, "lat", backward)
    return low, high


def split_pair(values):
    high = values.astype(jnp.bfloat16)
    rest = (values - high.astype(jnp.float32)).astype(jnp.bfloat16)
    return jnp.concatenate([high, rest], axis=-1)


def edges(values, width):
    return jnp.concatenate([values[:width], values[values.shape[0] - width :]], axis=0)


def side_lines(values):
    return jnp.concatenate([values[:, :HALO], values[:, values.shape[1] - HALO :]], axis=1)


def next_edges(state, low, high, inputs, *weights):
    lines = gru_lines(
        side_lines(state), side_lines(low), side_lines(high), side_lines(inputs), *weights
    )
    return lines.transpose(1, 0, 2)


def valid_conv(padded, weight, out_len):
    other = padded.shape[1]
    total = None
    for tap in range(5):
        piece = padded[tap : tap + out_len].reshape(-1, padded.shape[2])
        term = jnp.dot(piece, weight[tap], preferred_element_type=jnp.float32)
        total = term if total is None else total + term
    return total.reshape(out_len, other, -1)


def gru_lines(state, low, high, inputs, zr_weight, q_weight, z_bias, gate_row):
    hid = state.shape[2]
    size = state.shape[0]
    inner = size + 2 * (HALO - 2)
    wide_bf = jnp.concatenate(
        [low[..., :hid], state.astype(jnp.bfloat16), high[..., :hid]], axis=0
    )
    low_f = low[..., :hid].astype(jnp.float32) + low[..., hid:].astype(jnp.float32)
    high_f = high[..., :hid].astype(jnp.float32) + high[..., hid:].astype(jnp.float32)
    mid = jnp.concatenate([low_f[2:], state, high_f[: HALO - 2]], axis=0)
    mixed = valid_conv(wide_bf, zr_weight, inner)
    reset = jax.nn.sigmoid(inputs[..., hid : 2 * hid] + mixed[..., hid:] + gate_row[:hid])
    reset_state = (reset * mid).astype(jnp.bfloat16)
    core_x = inputs[HALO - 2 : HALO - 2 + size]
    core_mixed = mixed[HALO - 2 : HALO - 2 + size]
    update = jax.nn.sigmoid(core_x[..., :hid] + core_mixed[..., :hid] + z_bias)
    candidate = jnp.tanh(
        core_x[..., 2 * hid :] + valid_conv(reset_state, q_weight, size) + gate_row[hid:]
    )
    return (1.0 - update) * state + update * candidate


def gru_kernel(
    flip,
    state_ref,
    low_ref,
    high_ref,
    x_ref,
    zr_ref,
    q_ref,
    zb_ref,
    gr_ref,
    out_ref,
    wide,
    mid,
    reset_state,
    taps,
    reset_taps,
):
    hid = state_ref.shape[1]
    line = low_ref.shape[0] // HALO
    total = state_ref.shape[0]
    inner = total + 2 * (HALO - 2) * line
    state = state_ref[...]
    wide[: HALO * line] = low_ref[:, :hid]
    wide[HALO * line : HALO * line + total] = state.astype(jnp.bfloat16)
    wide[HALO * line + total :] = high_ref[:, :hid]
    side = (HALO - 2) * line
    mid[:side] = (
        low_ref[2 * line :, :hid].astype(jnp.float32) + low_ref[2 * line :, hid:].astype(jnp.float32)
    )
    mid[side : side + total] = state
    mid[side + total :] = (
        high_ref[:side, :hid].astype(jnp.float32) + high_ref[:side, hid:].astype(jnp.float32)
    )
    for tap in range(5):
        taps[:, tap * hid : (tap + 1) * hid] = wide[tap * line : tap * line + inner]
    mixed = jnp.dot(taps[...], zr_ref[...], preferred_element_type=jnp.float32)
    gate_row = gr_ref[...]
    reset = jax.nn.sigmoid(x_ref[:, hid : 2 * hid] + mixed[:, hid:] + gate_row[:, :hid])
    reset_state[...] = (reset * mid[...]).astype(jnp.bfloat16)
    for tap in range(5):
        reset_taps[:, tap * hid : (tap + 1) * hid] = reset_state[tap * line : tap * line + total]
    cand = jnp.dot(reset_taps[...], q_ref[...], preferred_element_type=jnp.float32)
    core_x = x_ref[side : side + total]
    update = jax.nn.sigmoid(core_x[:, :hid] + mixed[side : side + total, :hid] + zb_ref[...])
    candidate = jnp.tanh(core_x[:, 2 * hid :] + cand + gate_row[:, hid:])
    new = (1.0 - update) * state + update * candidate
    if out_ref.shape == state_ref.shape and not flip:
        out_ref[...] = new
    else:
        size = total // line
        for a in range(size):
            out_ref[pl.ds(a, line, stride=size)] = new[a * line : (a + 1) * line]


def gru_pass(state, low, high, inputs, zr_weight, q_weight, z_bias, gate_row, flip=True):
    size, line, hid = state.shape
    total = size * line
    inner = total + 2 * (HALO - 2) * line
    vmem = pl.BlockSpec(memory_space=pltpu.VMEM)
    out = pl.pallas_call(
        functools.partial(gru_kernel, flip),
        out_shape=jax.ShapeDtypeStruct((total, hid), jnp.float32),
        in_specs=[vmem] * 8,
        out_specs=vmem,
        scratch_shapes=[
            pltpu.VMEM((total + 2 * HALO * line, hid), jnp.bfloat16),
            pltpu.VMEM((inner, hid), jnp.float32),
            pltpu.VMEM((inner, hid), jnp.bfloat16),
            pltpu.VMEM((inner, 5 * hid), jnp.bfloat16),
            pltpu.VMEM((total, 5 * hid), jnp.bfloat16),
        ],
        cost_estimate=pl.CostEstimate(
            flops=2 * 5 * hid * (inner * 2 * hid + total * hid),
            transcendentals=inner * hid + 2 * total * hid,
            bytes_accessed=4 * (2 * total * hid + inner * 3 * hid),
        ),
    )(
        state.reshape(total, hid),
        low.reshape(HALO * line, 2 * hid),
        high.reshape(HALO * line, 2 * hid),
        inputs.reshape(inner, 3 * hid),
        zr_weight.reshape(5 * hid, 2 * hid),
        q_weight.reshape(5 * hid, hid),
        z_bias.reshape(1, hid),
        gate_row.reshape(1, 2 * hid),
    )
    if flip:
        return out.reshape(line, size, hid)
    return out.reshape(size, line, hid)


def local(
    feat_one,
    feat_two,
    context_in,
    hidden_init,
    corr_proj,
    input_conv,
    state_zr,
    state_q,
    update_bias,
    gate_bias,
    blk_offset,
    blk_class,
    blk_count,
):
    rows, cols, chans = feat_one.shape
    hid = hidden_init.shape[2]
    pool_rows = rows // POOLR
    pool_cols = cols // POOLC
    points = POOLR * POOLC
    cell = jnp.arange(rows * cols, dtype=jnp.int32)
    window = (cell // (cols * pool_rows)) * POOLC + (cell % cols) // pool_cols
    pool_mat = jnp.where(
        window[None, :] == jnp.arange(points, dtype=jnp.int32)[:, None],
        jnp.bfloat16(1.0 / (pool_rows * pool_cols)),
        jnp.bfloat16(0.0),
    )
    pooled = jnp.dot(
        pool_mat, feat_two.reshape(rows * cols, chans), preferred_element_type=jnp.float32
    ).astype(jnp.bfloat16)
    near = jnp.concatenate(
        [passed_along(pooled, "lon", 1), pooled, passed_along(pooled, "lon", -1)], axis=0
    )
    reach = 3
    keys = jnp.concatenate(
        [passed_along(near, "lon", reach), near, passed_along(near, "lon", -reach)], axis=0
    )

    queries = feat_one.reshape(rows * cols, chans)
    scale = chans ** (-0.5)
    corr = (
        lax.dot_general(queries, keys, (((1,), (1,)), ((), ())), preferred_element_type=jnp.float32)
        * scale
    ).astype(jnp.bfloat16)

    offsets = blk_offset[0, 0]
    classes = blk_class[0, 0]
    live = blk_count[0, 0]
    slots = offsets.shape[0]
    used = (jnp.arange(slots, dtype=jnp.int32) < live).astype(jnp.float32)
    by_offset = (offsets[None, :] + RMAX == jnp.arange(2 * RMAX + 1, dtype=jnp.int32)[:, None])
    by_class = classes[:, None] == jnp.arange(NCLASS, dtype=jnp.int32)[None, :]
    counts = jnp.dot(
        by_offset.astype(jnp.float32) * used[None, :],
        by_class.astype(jnp.float32),
        precision=lax.Precision.HIGHEST,
    )
    weight = jnp.einsum(
        "oc,cph->oph",
        counts.astype(jnp.bfloat16),
        corr_proj,
        preferred_element_type=jnp.float32,
    ).reshape((2 * RMAX + 1) * points, hid)
    weight_hi = weight.astype(jnp.bfloat16)
    weight_lo = (weight - weight_hi.astype(jnp.float32)).astype(jnp.bfloat16)
    both = jnp.dot(
        corr, jnp.concatenate([weight_hi, weight_lo], axis=1), preferred_element_type=jnp.float32
    )
    motion_sum = both[:, :hid] + both[:, hid:]
    motion = jnp.maximum(motion_sum, 0.0).astype(jnp.bfloat16).reshape(rows, cols, hid)
    joined = jnp.concatenate([context_in, motion], axis=2)
    chan_in = joined.shape[2]
    joined_t = joined.transpose(1, 0, 2)
    hidden_t = hidden_init.transpose(1, 0, 2)
    low, high = swap_lon(jnp.concatenate([joined_t, hidden_t], axis=2), HALO)
    x_lon = valid_conv(
        jnp.concatenate([low[..., :chan_in], joined_t, high[..., :chan_in]], axis=0),
        input_conv[0],
        cols + 2 * (HALO - 2),
    )
    nothing = jnp.zeros_like(low[..., chan_in:])
    state_low = jnp.concatenate([low[..., chan_in:], nothing], axis=2)
    state_high = jnp.concatenate([high[..., chan_in:], nothing], axis=2)
    state = hidden_t.astype(jnp.float32)
    x_lat = None
    for step in range(ITERS):
        lon_weights = (state_zr[0], state_q[0], update_bias[0], gate_bias[0])
        lat_weights = (state_zr[1], state_q[1], update_bias[1], gate_bias[1])
        sent = split_pair(next_edges(state, state_low, state_high, x_lon, *lon_weights))
        state = gru_pass(state, state_low, state_high, x_lon, *lon_weights)
        if x_lat is None:
            sent = jnp.concatenate([edges(joined, HALO), sent], axis=2)
            low, high = swap_lat(sent, HALO)
            x_lat = valid_conv(
                jnp.concatenate([low[..., :chan_in], joined, high[..., :chan_in]], axis=0),
                input_conv[1],
                rows + 2 * (HALO - 2),
            )
            state_low, state_high = low[..., chan_in:], high[..., chan_in:]
        else:
            state_low, state_high = swap_lat(sent, HALO)
        last = step == ITERS - 1
        if not last:
            sent = split_pair(next_edges(state, state_low, state_high, x_lat, *lat_weights))
        state = gru_pass(state, state_low, state_high, x_lat, *lat_weights, flip=not last)
        if not last:
            state_low, state_high = swap_lon(sent, HALO)
    return state.astype(jnp.bfloat16)


def solution(mesh):
    placed = (
        P("lat", "lon", None),
        P("lat", "lon", None),
        P("lat", "lon", None),
        P("lat", "lon", None),
        P(),
        P(),
        P(),
        P(),
        P(),
        P(),
        P("lat", "lon", None),
        P("lat", "lon", None),
        P("lat", "lon"),
    )
    return jax.shard_map(
        local, mesh=mesh, in_specs=placed, out_specs=P("lat", "lon", None), check_vma=False
    )
```

```python
import jax
import jax.numpy as jnp
from jax import lax
from jax.sharding import PartitionSpec as P

POOLR = 8
POOLC = 16
RMAX = 4
ITERS = 4
NCLASS = 8
HALO = 4


def passed_along(value, axis, steps):
    count = lax.axis_size(axis)
    pairs = [(source, (source + steps) % count) for source in range(count)]
    return lax.ppermute(value, axis, pairs)


def extended(block, axis, dim, width, periodic):
    count = lax.axis_size(axis)
    forward = [(i, i + 1) for i in range(count - 1)]
    if periodic:
        forward.append((count - 1, 0))
    backward = [(target, source) for source, target in forward]
    low = lax.ppermute(
        lax.slice_in_dim(block, block.shape[dim] - width, None, axis=dim), axis, forward
    )
    high = lax.ppermute(lax.slice_in_dim(block, 0, width, axis=dim), axis, backward)
    return jnp.concatenate([low, block, high], axis=dim)


def rim_lon(values, width):
    return extended(values, "lon", 0, width, True)


def rim_lat(values, width):
    count = lax.axis_size("lat")
    here = lax.axis_index("lat")
    forward = [(i, (i + 1) % count) for i in range(count)]
    backward = [(target, source) for source, target in forward]
    low = lax.ppermute(values[values.shape[0] - width :], "lat", forward)
    high = lax.ppermute(values[:width], "lat", backward)
    low = jnp.where(here > 0, low, jnp.zeros_like(low))
    high = jnp.where(here < count - 1, high, jnp.zeros_like(high))
    return jnp.concatenate([low, values, high], axis=0)


def valid_conv(padded, weight, out_len):
    other = padded.shape[1]
    total = None
    for tap in range(5):
        piece = padded[tap : tap + out_len].reshape(-1, padded.shape[2])
        term = jnp.dot(piece, weight[tap], preferred_element_type=jnp.float32)
        total = term if total is None else total + term
    return total.reshape(out_len, other, -1)


def gru_pass(state, inputs, rim, zr_weight, q_weight, z_bias, gate_row):
    hid = state.shape[2]
    size = state.shape[0]
    inner = size + 2 * (HALO - 2)
    wide = rim(state, HALO)
    mixed = valid_conv(wide.astype(jnp.bfloat16), zr_weight, inner)
    reset = jax.nn.sigmoid(inputs[..., hid : 2 * hid] + mixed[..., hid:] + gate_row[:hid])
    reset_state = (reset * wide[2 : 2 + inner]).astype(jnp.bfloat16)
    core_x = inputs[HALO - 2 : HALO - 2 + size]
    core_mixed = mixed[HALO - 2 : HALO - 2 + size]
    update = jax.nn.sigmoid(core_x[..., :hid] + core_mixed[..., :hid] + z_bias)
    candidate = jnp.tanh(
        core_x[..., 2 * hid :] + valid_conv(reset_state, q_weight, size) + gate_row[hid:]
    )
    return (1.0 - update) * state + update * candidate


def local(
    feat_one,
    feat_two,
    context_in,
    hidden_init,
    corr_proj,
    input_conv,
    state_zr,
    state_q,
    update_bias,
    gate_bias,
    blk_offset,
    blk_class,
    blk_count,
):
    rows, cols, chans = feat_one.shape
    hid = hidden_init.shape[2]
    pool_rows = rows // POOLR
    pool_cols = cols // POOLC
    points = POOLR * POOLC
    cell = jnp.arange(rows * cols, dtype=jnp.int32)
    window = (cell // (cols * pool_rows)) * POOLC + (cell % cols) // pool_cols
    pool_mat = jnp.where(
        window[None, :] == jnp.arange(points, dtype=jnp.int32)[:, None],
        jnp.bfloat16(1.0 / (pool_rows * pool_cols)),
        jnp.bfloat16(0.0),
    )
    pooled = jnp.dot(
        pool_mat, feat_two.reshape(rows * cols, chans), preferred_element_type=jnp.float32
    ).astype(jnp.bfloat16)
    near = jnp.concatenate(
        [passed_along(pooled, "lon", 1), pooled, passed_along(pooled, "lon", -1)], axis=0
    )
    reach = 3
    keys = jnp.concatenate(
        [passed_along(near, "lon", reach), near, passed_along(near, "lon", -reach)], axis=0
    )

    queries = feat_one.reshape(rows * cols, chans)
    scale = chans ** (-0.5)
    corr = (
        lax.dot_general(queries, keys, (((1,), (1,)), ((), ())), preferred_element_type=jnp.float32)
        * scale
    ).astype(jnp.bfloat16)

    offsets = blk_offset[0, 0]
    classes = blk_class[0, 0]
    live = blk_count[0, 0]
    slots = offsets.shape[0]
    used = (jnp.arange(slots, dtype=jnp.int32) < live).astype(jnp.float32)
    by_offset = (offsets[None, :] + RMAX == jnp.arange(2 * RMAX + 1, dtype=jnp.int32)[:, None])
    by_class = classes[:, None] == jnp.arange(NCLASS, dtype=jnp.int32)[None, :]
    counts = jnp.dot(
        by_offset.astype(jnp.float32) * used[None, :],
        by_class.astype(jnp.float32),
        precision=lax.Precision.HIGHEST,
    )
    weight = jnp.einsum(
        "oc,cph->oph",
        counts.astype(jnp.bfloat16),
        corr_proj,
        preferred_element_type=jnp.float32,
    ).reshape((2 * RMAX + 1) * points, hid)
    weight_hi = weight.astype(jnp.bfloat16)
    weight_lo = (weight - weight_hi.astype(jnp.float32)).astype(jnp.bfloat16)
    both = jnp.dot(
        corr, jnp.concatenate([weight_hi, weight_lo], axis=1), preferred_element_type=jnp.float32
    )
    motion_sum = both[:, :hid] + both[:, hid:]
    motion = jnp.maximum(motion_sum, 0.0).astype(jnp.bfloat16).reshape(rows, cols, hid)
    joined = jnp.concatenate([context_in, motion], axis=2)
    x_lon = valid_conv(
        rim_lon(joined.transpose(1, 0, 2), HALO), input_conv[0], cols + 2 * (HALO - 2)
    )
    x_lat = valid_conv(rim_lat(joined, HALO), input_conv[1], rows + 2 * (HALO - 2))
    def iteration(step, state):
        state = gru_pass(
            state.transpose(1, 0, 2),
            x_lon,
            rim_lon,
            state_zr[0],
            state_q[0],
            update_bias[0],
            gate_bias[0],
        ).transpose(1, 0, 2)
        return gru_pass(
            state, x_lat, rim_lat, state_zr[1], state_q[1], update_bias[1], gate_bias[1]
        )

    state = lax.fori_loop(0, ITERS, iteration, hidden_init.astype(jnp.float32))
    return state.astype(jnp.bfloat16)


def solution(mesh):
    placed = (
        P("lat", "lon", None),
        P("lat", "lon", None),
        P("lat", "lon", None),
        P("lat", "lon", None),
        P(),
        P(),
        P(),
        P(),
        P(),
        P(),
        P("lat", "lon", None),
        P("lat", "lon", None),
        P("lat", "lon"),
    )
    return jax.shard_map(
        local, mesh=mesh, in_specs=placed, out_specs=P("lat", "lon", None), check_vma=False
    )
```

```python
import jax
import jax.numpy as jnp
from jax import lax
from jax.sharding import PartitionSpec as P

POOLR = 8
POOLC = 16
RMAX = 4
ITERS = 4
NCLASS = 8
HALO = 4


def passed_along(value, axis, steps):
    count = lax.axis_size(axis)
    pairs = [(source, (source + steps) % count) for source in range(count)]
    return lax.ppermute(value, axis, pairs)


def extended(block, axis, dim, width, periodic):
    count = lax.axis_size(axis)
    forward = [(i, i + 1) for i in range(count - 1)]
    if periodic:
        forward.append((count - 1, 0))
    backward = [(target, source) for source, target in forward]
    low = lax.ppermute(
        lax.slice_in_dim(block, block.shape[dim] - width, None, axis=dim), axis, forward
    )
    high = lax.ppermute(lax.slice_in_dim(block, 0, width, axis=dim), axis, backward)
    return jnp.concatenate([low, block, high], axis=dim)


def rim_lon(values, width):
    return extended(values, "lon", 0, width, True)


def rim_lat(values, width):
    count = lax.axis_size("lat")
    here = lax.axis_index("lat")
    forward = [(i, (i + 1) % count) for i in range(count)]
    backward = [(target, source) for source, target in forward]
    last = values[values.shape[0] - width :]
    first = values[:width]
    last = jnp.where(here < count - 1, last, jnp.zeros_like(last))
    first = jnp.where(here > 0, first, jnp.zeros_like(first))
    low = lax.ppermute(last, "lat", forward)
    high = lax.ppermute(first, "lat", backward)
    return jnp.concatenate([low, values, high], axis=0)


def valid_conv(padded, weight, out_len):
    other = padded.shape[1]
    total = None
    for tap in range(5):
        piece = padded[tap : tap + out_len].reshape(-1, padded.shape[2])
        term = jnp.dot(piece, weight[tap], preferred_element_type=jnp.float32)
        total = term if total is None else total + term
    return total.reshape(out_len, other, -1)


def gru_pass(state, inputs, rim, zr_weight, q_weight, z_bias, gate_row):
    hid = state.shape[2]
    size = state.shape[0]
    inner = size + 2 * (HALO - 2)
    wide = rim(state, HALO)
    mixed = valid_conv(wide.astype(jnp.bfloat16), zr_weight, inner)
    reset = jax.nn.sigmoid(inputs[..., hid : 2 * hid] + mixed[..., hid:] + gate_row[:hid])
    reset_state = (reset * wide[2 : 2 + inner]).astype(jnp.bfloat16)
    core_x = inputs[HALO - 2 : HALO - 2 + size]
    core_mixed = mixed[HALO - 2 : HALO - 2 + size]
    update = jax.nn.sigmoid(core_x[..., :hid] + core_mixed[..., :hid] + z_bias)
    candidate = jnp.tanh(
        core_x[..., 2 * hid :] + valid_conv(reset_state, q_weight, size) + gate_row[hid:]
    )
    return (1.0 - update) * state + update * candidate


def local(
    feat_one,
    feat_two,
    context_in,
    hidden_init,
    corr_proj,
    input_conv,
    state_zr,
    state_q,
    update_bias,
    gate_bias,
    blk_offset,
    blk_class,
    blk_count,
):
    rows, cols, chans = feat_one.shape
    hid = hidden_init.shape[2]
    pool_rows = rows // POOLR
    pool_cols = cols // POOLC
    points = POOLR * POOLC
    cell = jnp.arange(rows * cols, dtype=jnp.int32)
    window = (cell // (cols * pool_rows)) * POOLC + (cell % cols) // pool_cols
    pool_mat = jnp.where(
        window[None, :] == jnp.arange(points, dtype=jnp.int32)[:, None],
        jnp.bfloat16(1.0 / (pool_rows * pool_cols)),
        jnp.bfloat16(0.0),
    )
    pooled = jnp.dot(
        pool_mat, feat_two.reshape(rows * cols, chans), preferred_element_type=jnp.float32
    ).astype(jnp.bfloat16)
    near = jnp.concatenate(
        [passed_along(pooled, "lon", 1), pooled, passed_along(pooled, "lon", -1)], axis=0
    )
    reach = 3
    queries = feat_one.reshape(rows * cols, chans)
    scale = chans ** (-0.5)

    def correlate(keys):
        return (
            lax.dot_general(
                queries, keys, (((1,), (1,)), ((), ())), preferred_element_type=jnp.float32
            )
            * scale
        ).astype(jnp.bfloat16)

    corr = jnp.concatenate(
        [
            correlate(passed_along(near, "lon", reach)),
            correlate(near),
            correlate(passed_along(near, "lon", -reach)),
        ],
        axis=1,
    )

    offsets = blk_offset[0, 0]
    classes = blk_class[0, 0]
    live = blk_count[0, 0]
    slots = offsets.shape[0]
    used = (jnp.arange(slots, dtype=jnp.int32) < live).astype(jnp.float32)
    by_offset = (offsets[None, :] + RMAX == jnp.arange(2 * RMAX + 1, dtype=jnp.int32)[:, None])
    by_class = classes[:, None] == jnp.arange(NCLASS, dtype=jnp.int32)[None, :]
    counts = jnp.dot(
        by_offset.astype(jnp.float32) * used[None, :],
        by_class.astype(jnp.float32),
        precision=lax.Precision.HIGHEST,
    )
    weight = jnp.einsum(
        "oc,cph->oph",
        counts.astype(jnp.bfloat16),
        corr_proj,
        preferred_element_type=jnp.float32,
    ).reshape((2 * RMAX + 1) * points, hid)
    weight_hi = weight.astype(jnp.bfloat16)
    weight_lo = (weight - weight_hi.astype(jnp.float32)).astype(jnp.bfloat16)
    both = jnp.dot(
        corr, jnp.concatenate([weight_hi, weight_lo], axis=1), preferred_element_type=jnp.float32
    )
    motion_sum = both[:, :hid] + both[:, hid:]
    motion = jnp.maximum(motion_sum, 0.0).astype(jnp.bfloat16).reshape(rows, cols, hid)
    joined = jnp.concatenate([context_in, motion], axis=2)
    x_lon = valid_conv(
        rim_lon(joined.transpose(1, 0, 2), HALO), input_conv[0], cols + 2 * (HALO - 2)
    )
    x_lat = valid_conv(rim_lat(joined, HALO), input_conv[1], rows + 2 * (HALO - 2))
    state = hidden_init.astype(jnp.float32)
    for step in range(ITERS):
        state = gru_pass(
            state.transpose(1, 0, 2),
            x_lon,
            rim_lon,
            state_zr[0],
            state_q[0],
            update_bias[0],
            gate_bias[0],
        ).transpose(1, 0, 2)
        state = gru_pass(
            state, x_lat, rim_lat, state_zr[1], state_q[1], update_bias[1], gate_bias[1]
        )
    return state.astype(jnp.bfloat16)


def solution(mesh):
    placed = (
        P("lat", "lon", None),
        P("lat", "lon", None),
        P("lat", "lon", None),
        P("lat", "lon", None),
        P(),
        P(),
        P(),
        P(),
        P(),
        P(),
        P("lat", "lon", None),
        P("lat", "lon", None),
        P("lat", "lon"),
    )
    return jax.shard_map(
        local, mesh=mesh, in_specs=placed, out_specs=P("lat", "lon", None), check_vma=False
    )
```

```python
import jax
import jax.numpy as jnp
from jax import lax
from jax.sharding import PartitionSpec as P

POOLR = 8
POOLC = 16
RMAX = 4
ITERS = 4
NCLASS = 8
HALO = 4


def passed_along(value, axis, steps):
    count = lax.axis_size(axis)
    pairs = [(source, (source + steps) % count) for source in range(count)]
    return lax.ppermute(value, axis, pairs)


def extended(block, axis, dim, width, periodic):
    count = lax.axis_size(axis)
    forward = [(i, i + 1) for i in range(count - 1)]
    if periodic:
        forward.append((count - 1, 0))
    backward = [(target, source) for source, target in forward]
    low = lax.ppermute(
        lax.slice_in_dim(block, block.shape[dim] - width, None, axis=dim), axis, forward
    )
    high = lax.ppermute(lax.slice_in_dim(block, 0, width, axis=dim), axis, backward)
    return jnp.concatenate([low, block, high], axis=dim)


def rim_lon(values, width):
    return extended(values, "lon", 0, width, True)


def rim_lat(values, width):
    count = lax.axis_size("lat")
    here = lax.axis_index("lat")
    forward = [(i, (i + 1) % count) for i in range(count)]
    backward = [(target, source) for source, target in forward]
    last = values[values.shape[0] - width :]
    first = values[:width]
    last = jnp.where(here < count - 1, last, jnp.zeros_like(last))
    first = jnp.where(here > 0, first, jnp.zeros_like(first))
    low = lax.ppermute(last, "lat", forward)
    high = lax.ppermute(first, "lat", backward)
    return jnp.concatenate([low, values, high], axis=0)


def valid_conv(padded, weight, out_len):
    other = padded.shape[1]
    total = None
    for tap in range(5):
        piece = padded[tap : tap + out_len].reshape(-1, padded.shape[2])
        term = jnp.dot(piece, weight[tap], preferred_element_type=jnp.float32)
        total = term if total is None else total + term
    return total.reshape(out_len, other, -1)


def gru_pass(state, inputs, rim, zr_weight, q_weight, z_bias, gate_row, wide=None):
    hid = state.shape[2]
    size = state.shape[0]
    inner = size + 2 * (HALO - 2)
    if wide is None:
        wide = rim(state, HALO)
    mixed = valid_conv(wide.astype(jnp.bfloat16), zr_weight, inner)
    reset = jax.nn.sigmoid(inputs[..., hid : 2 * hid] + mixed[..., hid:] + gate_row[:hid])
    reset_state = (reset * wide[2 : 2 + inner]).astype(jnp.bfloat16)
    core_x = inputs[HALO - 2 : HALO - 2 + size]
    core_mixed = mixed[HALO - 2 : HALO - 2 + size]
    update = jax.nn.sigmoid(core_x[..., :hid] + core_mixed[..., :hid] + z_bias)
    candidate = jnp.tanh(
        core_x[..., 2 * hid :] + valid_conv(reset_state, q_weight, size) + gate_row[hid:]
    )
    return (1.0 - update) * state + update * candidate


def local(
    feat_one,
    feat_two,
    context_in,
    hidden_init,
    corr_proj,
    input_conv,
    state_zr,
    state_q,
    update_bias,
    gate_bias,
    blk_offset,
    blk_class,
    blk_count,
):
    rows, cols, chans = feat_one.shape
    hid = hidden_init.shape[2]
    pool_rows = rows // POOLR
    pool_cols = cols // POOLC
    points = POOLR * POOLC
    cell = jnp.arange(rows * cols, dtype=jnp.int32)
    window = (cell // (cols * pool_rows)) * POOLC + (cell % cols) // pool_cols
    pool_mat = jnp.where(
        window[None, :] == jnp.arange(points, dtype=jnp.int32)[:, None],
        jnp.bfloat16(1.0 / (pool_rows * pool_cols)),
        jnp.bfloat16(0.0),
    )
    pooled = jnp.dot(
        pool_mat, feat_two.reshape(rows * cols, chans), preferred_element_type=jnp.float32
    ).astype(jnp.bfloat16)
    near = jnp.concatenate(
        [passed_along(pooled, "lon", 1), pooled, passed_along(pooled, "lon", -1)], axis=0
    )
    reach = 3
    queries = feat_one.reshape(rows * cols, chans)
    scale = chans ** (-0.5)

    def correlate(keys):
        return (
            lax.dot_general(
                queries, keys, (((1,), (1,)), ((), ())), preferred_element_type=jnp.float32
            )
            * scale
        ).astype(jnp.bfloat16)

    corr = jnp.concatenate(
        [
            correlate(passed_along(near, "lon", reach)),
            correlate(near),
            correlate(passed_along(near, "lon", -reach)),
        ],
        axis=1,
    )

    offsets = blk_offset[0, 0]
    classes = blk_class[0, 0]
    live = blk_count[0, 0]
    slots = offsets.shape[0]
    used = (jnp.arange(slots, dtype=jnp.int32) < live).astype(jnp.float32)
    by_offset = (offsets[None, :] + RMAX == jnp.arange(2 * RMAX + 1, dtype=jnp.int32)[:, None])
    by_class = classes[:, None] == jnp.arange(NCLASS, dtype=jnp.int32)[None, :]
    counts = jnp.dot(
        by_offset.astype(jnp.float32) * used[None, :],
        by_class.astype(jnp.float32),
        precision=lax.Precision.HIGHEST,
    )
    weight = jnp.einsum(
        "oc,cph->oph",
        counts.astype(jnp.bfloat16),
        corr_proj,
        preferred_element_type=jnp.float32,
    ).reshape((2 * RMAX + 1) * points, hid)
    weight_hi = weight.astype(jnp.bfloat16)
    weight_lo = (weight - weight_hi.astype(jnp.float32)).astype(jnp.bfloat16)
    both = jnp.dot(
        corr, jnp.concatenate([weight_hi, weight_lo], axis=1), preferred_element_type=jnp.float32
    )
    motion_sum = both[:, :hid] + both[:, hid:]
    motion = jnp.maximum(motion_sum, 0.0).astype(jnp.bfloat16).reshape(rows, cols, hid)
    joined = jnp.concatenate([context_in, motion], axis=2)
    chan_in = joined.shape[2]
    packed = rim_lon(
        jnp.concatenate([joined.transpose(1, 0, 2), hidden_init.transpose(1, 0, 2)], axis=2), HALO
    )
    x_lon = valid_conv(packed[..., :chan_in], input_conv[0], cols + 2 * (HALO - 2))
    x_lat = valid_conv(rim_lat(joined, HALO), input_conv[1], rows + 2 * (HALO - 2))
    state = hidden_init.astype(jnp.float32)
    for step in range(ITERS):
        state = gru_pass(
            state.transpose(1, 0, 2),
            x_lon,
            rim_lon,
            state_zr[0],
            state_q[0],
            update_bias[0],
            gate_bias[0],
            wide=packed[..., chan_in:].astype(jnp.float32) if step == 0 else None,
        ).transpose(1, 0, 2)
        state = gru_pass(
            state, x_lat, rim_lat, state_zr[1], state_q[1], update_bias[1], gate_bias[1]
        )
    return state.astype(jnp.bfloat16)


def solution(mesh):
    placed = (
        P("lat", "lon", None),
        P("lat", "lon", None),
        P("lat", "lon", None),
        P("lat", "lon", None),
        P(),
        P(),
        P(),
        P(),
        P(),
        P(),
        P("lat", "lon", None),
        P("lat", "lon", None),
        P("lat", "lon"),
    )
    return jax.shard_map(
        local, mesh=mesh, in_specs=placed, out_specs=P("lat", "lon", None), check_vma=False
    )
```

```python
import jax
import jax.numpy as jnp
from jax import lax
from jax.sharding import PartitionSpec as P

POOLR = 8
POOLC = 16
RMAX = 4
ITERS = 4
NCLASS = 8
HALO = 4


def passed_along(value, axis, steps):
    count = lax.axis_size(axis)
    pairs = [(source, (source + steps) % count) for source in range(count)]
    return lax.ppermute(value, axis, pairs)


def extended(block, axis, dim, width, periodic):
    count = lax.axis_size(axis)
    forward = [(i, i + 1) for i in range(count - 1)]
    if periodic:
        forward.append((count - 1, 0))
    backward = [(target, source) for source, target in forward]
    low = lax.ppermute(
        lax.slice_in_dim(block, block.shape[dim] - width, None, axis=dim), axis, forward
    )
    high = lax.ppermute(lax.slice_in_dim(block, 0, width, axis=dim), axis, backward)
    return jnp.concatenate([low, block, high], axis=dim)


def rim_lon(values, width):
    return extended(values, "lon", 0, width, True)


def rim_lat(values, width):
    low, high = swap_lat(values, width)
    return jnp.concatenate([low, values, high], axis=0)


def swap_lat(values, width):
    count = lax.axis_size("lat")
    here = lax.axis_index("lat")
    forward = [(i, (i + 1) % count) for i in range(count)]
    backward = [(target, source) for source, target in forward]
    last = values[values.shape[0] - width :]
    first = values[:width]
    last = jnp.where(here < count - 1, last, jnp.zeros_like(last))
    first = jnp.where(here > 0, first, jnp.zeros_like(first))
    low = lax.ppermute(last, "lat", forward)
    high = lax.ppermute(first, "lat", backward)
    return low, high


def edges(values, width):
    return jnp.concatenate([values[:width], values[values.shape[0] - width :]], axis=0)


def split_pair(values):
    high = values.astype(jnp.bfloat16)
    rest = (values - high.astype(jnp.float32)).astype(jnp.bfloat16)
    return jnp.concatenate([high, rest], axis=-1)


def joined_pair(pair):
    hid = pair.shape[-1] // 2
    return pair[..., :hid].astype(jnp.float32) + pair[..., hid:].astype(jnp.float32)


def valid_conv(padded, weight, out_len):
    other = padded.shape[1]
    total = None
    for tap in range(5):
        piece = padded[tap : tap + out_len].reshape(-1, padded.shape[2])
        term = jnp.dot(piece, weight[tap], preferred_element_type=jnp.float32)
        total = term if total is None else total + term
    return total.reshape(out_len, other, -1)


def gru_pass(state, inputs, rim, zr_weight, q_weight, z_bias, gate_row, wide=None):
    hid = state.shape[2]
    size = state.shape[0]
    inner = size + 2 * (HALO - 2)
    if wide is None:
        wide = rim(state, HALO)
    mixed = valid_conv(wide.astype(jnp.bfloat16), zr_weight, inner)
    reset = jax.nn.sigmoid(inputs[..., hid : 2 * hid] + mixed[..., hid:] + gate_row[:hid])
    reset_state = (reset * wide[2 : 2 + inner]).astype(jnp.bfloat16)
    core_x = inputs[HALO - 2 : HALO - 2 + size]
    core_mixed = mixed[HALO - 2 : HALO - 2 + size]
    update = jax.nn.sigmoid(core_x[..., :hid] + core_mixed[..., :hid] + z_bias)
    candidate = jnp.tanh(
        core_x[..., 2 * hid :] + valid_conv(reset_state, q_weight, size) + gate_row[hid:]
    )
    return (1.0 - update) * state + update * candidate


def local(
    feat_one,
    feat_two,
    context_in,
    hidden_init,
    corr_proj,
    input_conv,
    state_zr,
    state_q,
    update_bias,
    gate_bias,
    blk_offset,
    blk_class,
    blk_count,
):
    rows, cols, chans = feat_one.shape
    hid = hidden_init.shape[2]
    pool_rows = rows // POOLR
    pool_cols = cols // POOLC
    points = POOLR * POOLC
    cell = jnp.arange(rows * cols, dtype=jnp.int32)
    window = (cell // (cols * pool_rows)) * POOLC + (cell % cols) // pool_cols
    pool_mat = jnp.where(
        window[None, :] == jnp.arange(points, dtype=jnp.int32)[:, None],
        jnp.bfloat16(1.0 / (pool_rows * pool_cols)),
        jnp.bfloat16(0.0),
    )
    pooled = jnp.dot(
        pool_mat, feat_two.reshape(rows * cols, chans), preferred_element_type=jnp.float32
    ).astype(jnp.bfloat16)
    near = jnp.concatenate(
        [passed_along(pooled, "lon", 1), pooled, passed_along(pooled, "lon", -1)], axis=0
    )
    reach = 3
    queries = feat_one.reshape(rows * cols, chans)
    scale = chans ** (-0.5)

    def correlate(keys):
        return (
            lax.dot_general(
                queries, keys, (((1,), (1,)), ((), ())), preferred_element_type=jnp.float32
            )
            * scale
        ).astype(jnp.bfloat16)

    corr = jnp.concatenate(
        [
            correlate(passed_along(near, "lon", reach)),
            correlate(near),
            correlate(passed_along(near, "lon", -reach)),
        ],
        axis=1,
    )

    offsets = blk_offset[0, 0]
    classes = blk_class[0, 0]
    live = blk_count[0, 0]
    slots = offsets.shape[0]
    used = (jnp.arange(slots, dtype=jnp.int32) < live).astype(jnp.float32)
    by_offset = (offsets[None, :] + RMAX == jnp.arange(2 * RMAX + 1, dtype=jnp.int32)[:, None])
    by_class = classes[:, None] == jnp.arange(NCLASS, dtype=jnp.int32)[None, :]
    counts = jnp.dot(
        by_offset.astype(jnp.float32) * used[None, :],
        by_class.astype(jnp.float32),
        precision=lax.Precision.HIGHEST,
    )
    weight = jnp.einsum(
        "oc,cph->oph",
        counts.astype(jnp.bfloat16),
        corr_proj,
        preferred_element_type=jnp.float32,
    ).reshape((2 * RMAX + 1) * points, hid)
    weight_hi = weight.astype(jnp.bfloat16)
    weight_lo = (weight - weight_hi.astype(jnp.float32)).astype(jnp.bfloat16)
    both = jnp.dot(
        corr, jnp.concatenate([weight_hi, weight_lo], axis=1), preferred_element_type=jnp.float32
    )
    motion_sum = both[:, :hid] + both[:, hid:]
    motion = jnp.maximum(motion_sum, 0.0).astype(jnp.bfloat16).reshape(rows, cols, hid)
    joined = jnp.concatenate([context_in, motion], axis=2)
    chan_in = joined.shape[2]
    packed = rim_lon(
        jnp.concatenate([joined.transpose(1, 0, 2), hidden_init.transpose(1, 0, 2)], axis=2), HALO
    )
    x_lon = valid_conv(packed[..., :chan_in], input_conv[0], cols + 2 * (HALO - 2))
    x_lat = None
    state = hidden_init.astype(jnp.float32)
    for step in range(ITERS):
        state = gru_pass(
            state.transpose(1, 0, 2),
            x_lon,
            rim_lon,
            state_zr[0],
            state_q[0],
            update_bias[0],
            gate_bias[0],
            wide=packed[..., chan_in:].astype(jnp.float32) if step == 0 else None,
        ).transpose(1, 0, 2)
        wide = None
        if x_lat is None:
            sent = jnp.concatenate([edges(joined, HALO), split_pair(edges(state, HALO))], axis=2)
            low, high = swap_lat(sent, HALO)
            x_lat = valid_conv(
                jnp.concatenate([low[..., :chan_in], joined, high[..., :chan_in]], axis=0),
                input_conv[1],
                rows + 2 * (HALO - 2),
            )
            wide = jnp.concatenate(
                [joined_pair(low[..., chan_in:]), state, joined_pair(high[..., chan_in:])], axis=0
            )
        state = gru_pass(
            state, x_lat, rim_lat, state_zr[1], state_q[1], update_bias[1], gate_bias[1], wide=wide
        )
    return state.astype(jnp.bfloat16)


def solution(mesh):
    placed = (
        P("lat", "lon", None),
        P("lat", "lon", None),
        P("lat", "lon", None),
        P("lat", "lon", None),
        P(),
        P(),
        P(),
        P(),
        P(),
        P(),
        P("lat", "lon", None),
        P("lat", "lon", None),
        P("lat", "lon"),
    )
    return jax.shard_map(
        local, mesh=mesh, in_specs=placed, out_specs=P("lat", "lon", None), check_vma=False
    )
```

```python
import jax
import jax.numpy as jnp
from jax import lax
from jax.sharding import PartitionSpec as P

POOLR = 8
POOLC = 16
RMAX = 4
ITERS = 4
NCLASS = 8
HALO = 4


def passed_along(value, axis, steps):
    count = lax.axis_size(axis)
    pairs = [(source, (source + steps) % count) for source in range(count)]
    return lax.ppermute(value, axis, pairs)


def extended(block, axis, dim, width, periodic):
    count = lax.axis_size(axis)
    forward = [(i, i + 1) for i in range(count - 1)]
    if periodic:
        forward.append((count - 1, 0))
    backward = [(target, source) for source, target in forward]
    low = lax.ppermute(
        lax.slice_in_dim(block, block.shape[dim] - width, None, axis=dim), axis, forward
    )
    high = lax.ppermute(lax.slice_in_dim(block, 0, width, axis=dim), axis, backward)
    return jnp.concatenate([low, block, high], axis=dim)


def rim_lon(values, width):
    return extended(values, "lon", 0, width, True)


def rim_lat(values, width):
    count = lax.axis_size("lat")
    here = lax.axis_index("lat")
    forward = [(i, (i + 1) % count) for i in range(count)]
    backward = [(target, source) for source, target in forward]
    last = values[values.shape[0] - width :]
    first = values[:width]
    last = jnp.where(here < count - 1, last, jnp.zeros_like(last))
    first = jnp.where(here > 0, first, jnp.zeros_like(first))
    low = lax.ppermute(last, "lat", forward)
    high = lax.ppermute(first, "lat", backward)
    return jnp.concatenate([low, values, high], axis=0)


def valid_conv(padded, weight, out_len):
    other = padded.shape[1]
    total = None
    for tap in range(5):
        piece = padded[tap : tap + out_len].reshape(-1, padded.shape[2])
        term = jnp.dot(piece, weight[tap], preferred_element_type=jnp.float32)
        total = term if total is None else total + term
    return total.reshape(out_len, other, -1)


def gru_pass(state, inputs, rim, zr_weight, q_weight, z_bias, gate_row, wide=None):
    hid = state.shape[2]
    size = state.shape[0]
    inner = size + 2 * (HALO - 2)
    if wide is None:
        wide = rim(state, HALO)
    mixed = valid_conv(wide.astype(jnp.bfloat16), zr_weight, inner)
    reset = jax.nn.sigmoid(inputs[..., hid : 2 * hid] + mixed[..., hid:] + gate_row[:hid])
    reset_state = (reset * wide[2 : 2 + inner]).astype(jnp.bfloat16)
    core_x = inputs[HALO - 2 : HALO - 2 + size]
    core_mixed = mixed[HALO - 2 : HALO - 2 + size]
    update = jax.nn.sigmoid(core_x[..., :hid] + core_mixed[..., :hid] + z_bias)
    candidate = jnp.tanh(
        core_x[..., 2 * hid :] + valid_conv(reset_state, q_weight, size) + gate_row[hid:]
    )
    return (1.0 - update) * state + update * candidate


def local(
    feat_one,
    feat_two,
    context_in,
    hidden_init,
    corr_proj,
    input_conv,
    state_zr,
    state_q,
    update_bias,
    gate_bias,
    blk_offset,
    blk_class,
    blk_count,
):
    rows, cols, chans = feat_one.shape
    hid = hidden_init.shape[2]
    pool_rows = rows // POOLR
    pool_cols = cols // POOLC
    points = POOLR * POOLC
    cell = jnp.arange(rows * cols, dtype=jnp.int32)
    window = (cell // (cols * pool_rows)) * POOLC + (cell % cols) // pool_cols
    pool_mat = jnp.where(
        window[None, :] == jnp.arange(points, dtype=jnp.int32)[:, None],
        jnp.bfloat16(1.0 / (pool_rows * pool_cols)),
        jnp.bfloat16(0.0),
    )
    pooled = jnp.dot(
        pool_mat, feat_two.reshape(rows * cols, chans), preferred_element_type=jnp.float32
    ).astype(jnp.bfloat16)
    near = jnp.concatenate(
        [passed_along(pooled, "lon", 1), pooled, passed_along(pooled, "lon", -1)], axis=0
    )
    reach = 3
    queries = feat_one.reshape(rows * cols, chans)
    scale = chans ** (-0.5)

    def correlate(keys):
        return (
            lax.dot_general(
                queries, keys, (((1,), (1,)), ((), ())), preferred_element_type=jnp.float32
            )
            * scale
        ).astype(jnp.bfloat16)

    corr = jnp.concatenate(
        [
            correlate(passed_along(near, "lon", reach)),
            correlate(near),
            correlate(passed_along(near, "lon", -reach)),
        ],
        axis=1,
    )

    offsets = blk_offset[0, 0]
    classes = blk_class[0, 0]
    live = blk_count[0, 0]
    slots = offsets.shape[0]
    used = (jnp.arange(slots, dtype=jnp.int32) < live).astype(jnp.float32)
    by_offset = (offsets[None, :] + RMAX == jnp.arange(2 * RMAX + 1, dtype=jnp.int32)[:, None])
    by_class = classes[:, None] == jnp.arange(NCLASS, dtype=jnp.int32)[None, :]
    counts = jnp.dot(
        by_offset.astype(jnp.float32) * used[None, :],
        by_class.astype(jnp.float32),
        precision=lax.Precision.HIGHEST,
    )
    weight = jnp.einsum(
        "oc,cph->oph",
        counts.astype(jnp.bfloat16),
        corr_proj,
        preferred_element_type=jnp.float32,
    ).reshape((2 * RMAX + 1) * points, hid)
    weight_hi = weight.astype(jnp.bfloat16)
    weight_lo = (weight - weight_hi.astype(jnp.float32)).astype(jnp.bfloat16)
    both = jnp.dot(
        corr, jnp.concatenate([weight_hi, weight_lo], axis=1), preferred_element_type=jnp.float32
    )
    motion_sum = both[:, :hid] + both[:, hid:]
    motion = jnp.maximum(motion_sum, 0.0).astype(jnp.bfloat16).reshape(rows, cols, hid)
    joined = jnp.concatenate([context_in, motion], axis=2)
    chan_in = joined.shape[2]
    packed = rim_lon(
        jnp.concatenate([joined.transpose(1, 0, 2), hidden_init.transpose(1, 0, 2)], axis=2), HALO
    )
    x_lon = valid_conv(packed[..., :chan_in], input_conv[0], cols + 2 * (HALO - 2))
    x_lat = None
    state = hidden_init.astype(jnp.float32)
    for step in range(ITERS):
        state = gru_pass(
            state.transpose(1, 0, 2),
            x_lon,
            rim_lon,
            state_zr[0],
            state_q[0],
            update_bias[0],
            gate_bias[0],
            wide=packed[..., chan_in:].astype(jnp.float32) if step == 0 else None,
        ).transpose(1, 0, 2)
        if x_lat is None:
            late, state = lax.optimization_barrier((joined, state))
            x_lat = valid_conv(rim_lat(late, HALO), input_conv[1], rows + 2 * (HALO - 2))
        state = gru_pass(
            state, x_lat, rim_lat, state_zr[1], state_q[1], update_bias[1], gate_bias[1]
        )
    return state.astype(jnp.bfloat16)


def solution(mesh):
    placed = (
        P("lat", "lon", None),
        P("lat", "lon", None),
        P("lat", "lon", None),
        P("lat", "lon", None),
        P(),
        P(),
        P(),
        P(),
        P(),
        P(),
        P("lat", "lon", None),
        P("lat", "lon", None),
        P("lat", "lon"),
    )
    return jax.shard_map(
        local, mesh=mesh, in_specs=placed, out_specs=P("lat", "lon", None), check_vma=False
    )
```

```python
import jax
import jax.numpy as jnp
from jax import lax
from jax.sharding import PartitionSpec as P

POOLR = 8
POOLC = 16
RMAX = 4
ITERS = 4
NCLASS = 8
HALO = 4


def passed_along(value, axis, steps):
    count = lax.axis_size(axis)
    pairs = [(source, (source + steps) % count) for source in range(count)]
    return lax.ppermute(value, axis, pairs)


def extended(block, axis, dim, width, periodic):
    count = lax.axis_size(axis)
    forward = [(i, i + 1) for i in range(count - 1)]
    if periodic:
        forward.append((count - 1, 0))
    backward = [(target, source) for source, target in forward]
    low = lax.ppermute(
        lax.slice_in_dim(block, block.shape[dim] - width, None, axis=dim), axis, forward
    )
    high = lax.ppermute(lax.slice_in_dim(block, 0, width, axis=dim), axis, backward)
    return jnp.concatenate([low, block, high], axis=dim)


def rim_lon(values, width):
    return extended(values, "lon", 0, width, True)


def rim_lat(values, width):
    count = lax.axis_size("lat")
    here = lax.axis_index("lat")
    forward = [(i, (i + 1) % count) for i in range(count)]
    backward = [(target, source) for source, target in forward]
    last = values[values.shape[0] - width :]
    first = values[:width]
    last = jnp.where(here < count - 1, last, jnp.zeros_like(last))
    first = jnp.where(here > 0, first, jnp.zeros_like(first))
    low = lax.ppermute(last, "lat", forward)
    high = lax.ppermute(first, "lat", backward)
    return jnp.concatenate([low, values, high], axis=0)


def valid_conv(padded, weight, out_len):
    other = padded.shape[1]
    total = None
    for tap in range(5):
        piece = padded[tap : tap + out_len].reshape(-1, padded.shape[2])
        term = jnp.dot(piece, weight[tap], preferred_element_type=jnp.float32)
        total = term if total is None else total + term
    return total.reshape(out_len, other, -1)


def gru_pass(state, inputs, rim, zr_weight, q_weight, z_bias, gate_row, wide=None):
    hid = state.shape[2]
    size = state.shape[0]
    inner = size + 2 * (HALO - 2)
    if wide is None:
        wide = rim(state, HALO)
    mixed = valid_conv(wide.astype(jnp.bfloat16), zr_weight, inner)
    reset = jax.nn.sigmoid(inputs[..., hid : 2 * hid] + mixed[..., hid:] + gate_row[:hid])
    reset_state = (reset * wide[2 : 2 + inner]).astype(jnp.bfloat16)
    core_x = inputs[HALO - 2 : HALO - 2 + size]
    core_mixed = mixed[HALO - 2 : HALO - 2 + size]
    update = jax.nn.sigmoid(core_x[..., :hid] + core_mixed[..., :hid] + z_bias)
    candidate = jnp.tanh(
        core_x[..., 2 * hid :] + valid_conv(reset_state, q_weight, size) + gate_row[hid:]
    )
    return (1.0 - update) * state + update * candidate


def local(
    feat_one,
    feat_two,
    context_in,
    hidden_init,
    corr_proj,
    input_conv,
    state_zr,
    state_q,
    update_bias,
    gate_bias,
    blk_offset,
    blk_class,
    blk_count,
):
    rows, cols, chans = feat_one.shape
    hid = hidden_init.shape[2]
    pool_rows = rows // POOLR
    pool_cols = cols // POOLC
    points = POOLR * POOLC
    cell = jnp.arange(rows * cols, dtype=jnp.int32)
    window = (cell // (cols * pool_rows)) * POOLC + (cell % cols) // pool_cols
    pool_mat = jnp.where(
        window[None, :] == jnp.arange(points, dtype=jnp.int32)[:, None],
        jnp.bfloat16(1.0 / (pool_rows * pool_cols)),
        jnp.bfloat16(0.0),
    )
    pooled = jnp.dot(
        pool_mat, feat_two.reshape(rows * cols, chans), preferred_element_type=jnp.float32
    ).astype(jnp.bfloat16)
    near = jnp.concatenate(
        [passed_along(pooled, "lon", 1), pooled, passed_along(pooled, "lon", -1)], axis=0
    )
    reach = 3
    queries = feat_one.reshape(rows * cols, chans)
    scale = chans ** (-0.5)

    def correlate(keys):
        return (
            lax.dot_general(
                queries, keys, (((1,), (1,)), ((), ())), preferred_element_type=jnp.float32
            )
            * scale
        ).astype(jnp.bfloat16)

    groups = [
        correlate(passed_along(near, "lon", reach)),
        correlate(near),
        correlate(passed_along(near, "lon", -reach)),
    ]

    offsets = blk_offset[0, 0]
    classes = blk_class[0, 0]
    live = blk_count[0, 0]
    slots = offsets.shape[0]
    used = (jnp.arange(slots, dtype=jnp.int32) < live).astype(jnp.float32)
    by_offset = (offsets[None, :] + RMAX == jnp.arange(2 * RMAX + 1, dtype=jnp.int32)[:, None])
    by_class = classes[:, None] == jnp.arange(NCLASS, dtype=jnp.int32)[None, :]
    counts = jnp.dot(
        by_offset.astype(jnp.float32) * used[None, :],
        by_class.astype(jnp.float32),
        precision=lax.Precision.HIGHEST,
    )
    weight = jnp.einsum(
        "oc,cph->oph",
        counts.astype(jnp.bfloat16),
        corr_proj,
        preferred_element_type=jnp.float32,
    ).reshape((2 * RMAX + 1) * points, hid)
    weight_hi = weight.astype(jnp.bfloat16)
    weight_lo = (weight - weight_hi.astype(jnp.float32)).astype(jnp.bfloat16)
    paired = jnp.concatenate([weight_hi, weight_lo], axis=1)
    span = 3 * points
    both = jnp.dot(groups[1], paired[span : 2 * span], preferred_element_type=jnp.float32)
    for part in (0, 2):
        both = both + jnp.dot(
            groups[part], paired[part * span : (part + 1) * span], preferred_element_type=jnp.float32
        )
    motion_sum = both[:, :hid] + both[:, hid:]
    motion = jnp.maximum(motion_sum, 0.0).astype(jnp.bfloat16).reshape(rows, cols, hid)
    joined = jnp.concatenate([context_in, motion], axis=2)
    chan_in = joined.shape[2]
    packed = rim_lon(
        jnp.concatenate([joined.transpose(1, 0, 2), hidden_init.transpose(1, 0, 2)], axis=2), HALO
    )
    x_lon = valid_conv(packed[..., :chan_in], input_conv[0], cols + 2 * (HALO - 2))
    x_lat = valid_conv(rim_lat(joined, HALO), input_conv[1], rows + 2 * (HALO - 2))
    state = hidden_init.astype(jnp.float32)
    for step in range(ITERS):
        state = gru_pass(
            state.transpose(1, 0, 2),
            x_lon,
            rim_lon,
            state_zr[0],
            state_q[0],
            update_bias[0],
            gate_bias[0],
            wide=packed[..., chan_in:].astype(jnp.float32) if step == 0 else None,
        ).transpose(1, 0, 2)
        state = gru_pass(
            state, x_lat, rim_lat, state_zr[1], state_q[1], update_bias[1], gate_bias[1]
        )
    return state.astype(jnp.bfloat16)


def solution(mesh):
    placed = (
        P("lat", "lon", None),
        P("lat", "lon", None),
        P("lat", "lon", None),
        P("lat", "lon", None),
        P(),
        P(),
        P(),
        P(),
        P(),
        P(),
        P("lat", "lon", None),
        P("lat", "lon", None),
        P("lat", "lon"),
    )
    return jax.shard_map(
        local, mesh=mesh, in_specs=placed, out_specs=P("lat", "lon", None), check_vma=False
    )
```
